256 devices in a mesh: seq: 32 (over x, z), tp: 8 (over y, core).
Axes of the slice: x: 4, y: 4, z: 8, core: 2. Of those that a mesh axis runs over, the one named last changes fastest.
Arguments:
- tokens: bfloat16 [32768, 2048], P('seq', 'tp'), may hold values from -6 to 6
- w_inner: bfloat16 [2048, 2, 4096], P('seq', None, 'tp'), may hold values from -0.125 to 0.125
- w_states: bfloat16 [2048, 256], P('seq'), may hold values from -0.125 to 0.125
- w_step: bfloat16 [2048, 64], P('seq', 'tp'), may hold values from -0.125 to 0.125
- conv_inner: float32 [4, 4096], P(None, 'tp'), may hold values from -3 to 3
- conv_states: float32 [4, 256], replicated, may hold values from -3 to 3
- decay_rate: float32 [64], P('tp'), may hold values from 0 to 1, as said below
- step_bias: float32 [64], P('tp'), may hold values from -1 to 0.5
- skip_gain: float32 [64], P('tp'), may hold values from 0.5 to 1.5
- norm_gain: float32 [4096], P('tp'), may hold values from 0.5 to 1.5
- w_output: bfloat16 [4096, 2048], P('tp', 'seq'), may hold values from -0.09375 to 0.09375
- block_owner: int32 [128], replicated, may hold values from 0 to 19, as said below
- lengths: int32 [20], replicated, may hold values from 1 to 16384, as said below
Outputs:
- mixed: bfloat16 [32768, 2048], P('seq', 'tp')
The draws below stay inside these ranges and needn't reach their ends.
Inputs may be any that keep to these rules, and one draw needn't show every extreme that they name: `block_owner`: each prompt's blocks are consecutive, prompt r has ceil(lengths[r] / 256) of them, and the prompts follow one another in an order drawn afresh; one prompt has 64 blocks and is neither the first nor the last in that order. `lengths`: one prompt has exactly 16384 tokens. `decay_rate`: Positive.
All inputs are finite; a program needn't handle non-finite values.
Results may differ from the reference program's by a relative error of at most 0.0075.
Values may be sent and summed in bfloat16 or wider, within the bound.
No kernel may reach another device: no remote copies, remote signals or barrier semaphores. Data moves between devices by JAX's collectives and lax.ppermute only.
A program may use at most 64 MiB of HBM per device.

```python
import math
import jax
import jax.numpy as jnp
from jax import lax

D = 2048
HEADS = 64
HDIM = 64
INNER = 4096
STATE = 128
KCONV = 4
BLOCK = 256
NBLOCK = 128
TOKENS = 32768
REQ = 20
MAXBLK = 64


def request_plan(key):
    base_key = jax.random.fold_in(key, 17)
    key_long, key_pick, key_order, key_tail, key_place = jax.random.split(base_key, 5)
    longest = jax.random.randint(key_long, (), 0, REQ)
    spare_blocks = NBLOCK - MAXBLK - (REQ - 1)
    picked = jax.random.randint(key_pick, (spare_blocks,), 0, REQ - 1)
    picked = picked + (picked >= longest).astype(jnp.int32)
    request_ids = jnp.arange(REQ, dtype=jnp.int32)
    counts = 1 + jnp.sum((picked[:, None] == request_ids[None, :]).astype(jnp.int32), axis=0)
    counts = jnp.where(request_ids == longest, MAXBLK, counts)
    shuffled = jax.random.permutation(key_order, REQ).astype(jnp.int32)
    place_long = jax.random.randint(key_place, (), 1, REQ - 1)
    where_long = jnp.sum(jnp.where(shuffled == longest, request_ids, 0))
    moved = shuffled[place_long]
    request_order = jnp.where(request_ids == place_long, longest, jnp.where(request_ids == where_long, moved, shuffled))
    order_ends = jnp.cumsum(counts[request_order])
    block_ids = jnp.arange(NBLOCK, dtype=jnp.int32)
    placed = jnp.sum((order_ends[None, :] <= block_ids[:, None]).astype(jnp.int32), axis=1)
    owners = request_order[placed].astype(jnp.int32)
    tail_lengths = jax.random.randint(key_tail, (REQ,), 1, BLOCK + 1)
    tail_lengths = jnp.where(request_ids == longest, BLOCK, tail_lengths)
    lengths = (counts - 1) * BLOCK + tail_lengths
    return (owners, lengths.astype(jnp.int32))


def draw_block_owner(key, part):
    return request_plan(key)[0]


def draw_lengths(key, part):
    return request_plan(key)[1]


def draw_decay_rate(key, part):
    key_kind, key_slow, key_fast = jax.random.split(jax.random.fold_in(key, 29), 3)
    fast_heads = jax.random.randint(key_kind, (HEADS,), 0, 2) == 1
    chain_span = float(MAXBLK * BLOCK)
    slow_rates = jnp.exp(jax.random.uniform(key_slow, (HEADS,), jnp.float32, math.log(0.2), math.log(2.0))) / chain_span
    fast_rates = jnp.exp(jax.random.uniform(key_fast, (HEADS,), jnp.float32, math.log(0.03), math.log(0.05)))
    return jnp.where(fast_heads, fast_rates, slow_rates).astype(jnp.float32)


def levels(own_key, dims, cuts, smallest, top_value):
    gain, own = 1.0, jax.random.fold_in(own_key, 6)
    for dim, parts in cuts:
        heights = jnp.exp(jax.random.uniform(jax.random.fold_in(own, dim), (parts,), jnp.float32, smallest / len(cuts), top_value / len(cuts)))
        gain = gain * jnp.repeat(heights, dims[dim] // parts).reshape([-1 if axis == dim else 1 for axis in range(len(dims))])
    return gain


def normal_values(rng, shape, width, most, cuts=(), kind=jnp.bfloat16):
    factor_of = levels(rng, shape, cuts, -0.22, 0.18) if cuts else 1.0
    result = jax.random.normal(rng, shape, jnp.float32) * width * factor_of
    return jnp.minimum(jnp.maximum(result, -most), most).astype(kind)


def setup_inputs(seed: int = 0) -> dict:
    key_list = jax.random.split(jax.random.key(seed), 14)
    tokens = normal_values(key_list[0], (TOKENS, D), 1.0, 6.0, ((0, 32), (1, 8)))
    w_inner = normal_values(key_list[1], (D, 2, INNER), D ** -0.5, 0.125, ((0, 32), (2, 8)))
    w_states = normal_values(key_list[2], (D, 2 * STATE), D ** -0.5, 0.125, ((0, 32),))
    w_step = normal_values(key_list[3], (D, HEADS), D ** -0.5, 0.125, ((0, 32), (1, 8)))
    conv_inner = normal_values(key_list[4], (KCONV, INNER), KCONV ** -0.5, 3.0, ((1, 8),), jnp.float32)
    conv_states = normal_values(key_list[5], (KCONV, 2 * STATE), KCONV ** -0.5, 3.0, (), jnp.float32)
    decay_rate = draw_decay_rate(jax.random.fold_in(key_list[13], 71), 0)
    step_bias = jnp.clip(-1.0 + 1.5 * jax.random.uniform(key_list[7], (HEADS,), jnp.float32) ** levels(key_list[7], (HEADS,), ((0, 8),), -0.2, 0.2), -1.0, 0.5)
    skip_gain = jnp.clip(0.5 + 1.0 * jax.random.uniform(key_list[8], (HEADS,), jnp.float32) ** levels(key_list[8], (HEADS,), ((0, 8),), -0.2, 0.2), 0.5, 1.5)
    norm_gain = jnp.clip(0.5 + 1.0 * jax.random.uniform(key_list[9], (INNER,), jnp.float32) ** levels(key_list[9], (INNER,), ((0, 8),), -0.2, 0.2), 0.5, 1.5)
    w_output = normal_values(key_list[10], (INNER, D), INNER ** -0.5, 0.09375, ((0, 8), (1, 32)))
    block_owner = draw_block_owner(jax.random.fold_in(key_list[13], 71), 0)
    lengths = draw_lengths(jax.random.fold_in(key_list[13], 71), 0)
    return dict(tokens=tokens, w_inner=w_inner, w_states=w_states, w_step=w_step, conv_inner=conv_inner, conv_states=conv_states, decay_rate=decay_rate, step_bias=step_bias, skip_gain=skip_gain, norm_gain=norm_gain, w_output=w_output, block_owner=block_owner, lengths=lengths)


best_precision = lax.Precision.HIGHEST

def to_half(values):
    return lax.optimization_barrier(values.astype(jnp.bfloat16)).astype(jnp.float32)

def block_tables(block_owner, lengths):
    block_ids = jnp.arange(NBLOCK, dtype=jnp.int32)
    same_owner = block_owner[:, None] == block_owner[None, :]
    first_block = lax.optimization_barrier(jnp.min(jnp.where(same_owner, block_ids[None, :], NBLOCK), axis=1))
    starting = first_block == block_ids
    request_ids = jnp.arange(REQ, dtype=jnp.int32)
    own_length = lax.optimization_barrier(jnp.sum(jnp.where(block_owner[:, None] == request_ids[None, :], lengths[None, :], 0), axis=1))
    valid_rows = jnp.clip(own_length - (block_ids - first_block) * BLOCK, 0, BLOCK)
    return (starting, valid_rows)

def convolve(values, weights, in_block, carry_on):
    widened = values.astype(jnp.float32)
    total = jnp.zeros(values.shape, jnp.float32)
    for offset in range(KCONV):
        shifted = jnp.pad(widened, ((offset, 0), (0, 0)))[:values.shape[0]]
        keeping = (in_block >= offset) | carry_on
        total = total + jnp.where(keeping[:, None], shifted, 0.0) * weights[offset]
    return jax.nn.silu(total).astype(jnp.bfloat16)

def block_step(previous, inputs):
    x_block, b_block, c_block, log_block, step_block, starting = inputs
    cumulative = jnp.cumsum(log_block, axis=0)
    causal = jnp.arange(BLOCK)[:, None] >= jnp.arange(BLOCK)[None, :]
    spread = cumulative[:, None, :] - cumulative[None, :, :]
    decays = jnp.exp(jnp.where(causal[:, :, None], spread, -jnp.inf))
    intersection = jnp.einsum('in,jn->ij', c_block, b_block, precision=best_precision)
    mixing = to_half(decays * intersection[:, :, None] * step_block[None, :, :])
    y_inner = jnp.einsum('ijh,jhp->ihp', mixing, x_block, precision=best_precision)
    incoming = previous * jnp.where(starting, 0.0, 1.0)
    final_log = cumulative[-1]
    y_carry = jnp.exp(cumulative)[:, :, None] * jnp.einsum('in,hnp->ihp', c_block, to_half(incoming), precision=best_precision)
    tail_weight = jnp.exp(final_log[None, :] - cumulative) * step_block
    weighted_b = to_half(tail_weight[:, :, None] * b_block[:, None, :])
    fresh = jnp.einsum('jhn,jhp->hnp', weighted_b, x_block, precision=best_precision)
    state = jnp.exp(final_log)[:, None, None] * incoming + fresh
    return (state, y_inner + y_carry)

def reference(tokens, w_inner, w_states, w_step, conv_inner, conv_states, decay_rate, step_bias, skip_gain, norm_gain, w_output, block_owner, lengths):
    starting, valid_rows = block_tables(block_owner, lengths)
    projected = jnp.dot(tokens, w_inner.reshape(D, 2 * INNER), preferred_element_type=jnp.float32).astype(jnp.bfloat16)
    gate_in = projected[:, :INNER]
    x_in = projected[:, INNER:]
    bc_in = jnp.dot(tokens, w_states, preferred_element_type=jnp.float32).astype(jnp.bfloat16)
    step_raw = jnp.dot(tokens, w_step, preferred_element_type=jnp.float32).astype(jnp.bfloat16)
    positions = jnp.arange(TOKENS, dtype=jnp.int32)
    in_block = positions % BLOCK
    block_of = positions // BLOCK
    carry_on = jnp.logical_not(starting[block_of])
    x_conv = convolve(x_in, conv_inner, in_block, carry_on)
    bc_conv = convolve(bc_in, conv_states, in_block, carry_on)
    step_size = jax.nn.softplus(step_raw.astype(jnp.float32) + step_bias)
    log_decay = -decay_rate * step_size
    x_heads = x_conv.astype(jnp.float32).reshape(NBLOCK, BLOCK, HEADS, HDIM)
    b_rows = bc_conv[:, :STATE].astype(jnp.float32).reshape(NBLOCK, BLOCK, STATE)
    c_rows = bc_conv[:, STATE:].astype(jnp.float32).reshape(NBLOCK, BLOCK, STATE)
    initial = jnp.zeros((HEADS, STATE, HDIM), jnp.float32)
    _, y_blocks = lax.scan(block_step, initial, (x_heads, b_rows, c_rows, log_decay.reshape(NBLOCK, BLOCK, HEADS), step_size.reshape(NBLOCK, BLOCK, HEADS), starting))
    y_total = y_blocks.reshape(TOKENS, INNER) + jnp.repeat(skip_gain, HDIM)[None, :] * x_conv.astype(jnp.float32)
    gated = y_total * jax.nn.silu(gate_in.astype(jnp.float32))
    square_mean = lax.optimization_barrier(jnp.sum(gated * gated, axis=1)) / INNER
    normed = (gated * lax.rsqrt(square_mean + 1e-05)[:, None] * norm_gain).astype(jnp.bfloat16)
    mixed = jnp.dot(normed, w_output, preferred_element_type=jnp.float32)
    live = in_block < valid_rows[block_of]
    return jnp.where(live[:, None], mixed, 0.0).astype(jnp.bfloat16)
```

```python
import jax
import jax.numpy as jnp
from jax import lax
from jax.sharding import PartitionSpec as P

BLOCK = 256


def passed_along(value, axis, by):
    count = lax.axis_size(axis)
    pairs = [(i, i + by) for i in range(count) if 0 <= i + by < count]
    return lax.ppermute(value, axis, pairs)


def convolve(values, edge_rows, weights, in_block, carry_on):
    lag_rows = weights.shape[0] - 1
    row_total = values.shape[0]
    widened = jnp.concatenate([edge_rows, values], axis=0).astype(jnp.float32)
    total = jnp.zeros(values.shape, jnp.float32)
    for offset in range(weights.shape[0]):
        shifted = widened[lag_rows - offset : lag_rows - offset + row_total]
        keeping = (in_block >= offset) | carry_on
        total = total + jnp.where(keeping[:, None], shifted, 0.0) * weights[offset]
    return jax.nn.silu(total).astype(jnp.bfloat16)


def on_device(
    tokens,
    w_inner,
    w_states,
    w_step,
    conv_inner,
    conv_states,
    decay_rate,
    step_bias,
    skip_gain,
    norm_gain,
    w_output,
    block_owner,
    lengths,
):
    row_count = tokens.shape[0]
    local_blocks = row_count // BLOCK
    total_blocks = block_owner.shape[0]
    heads_here = w_step.shape[1]
    inner_here = w_inner.shape[2]
    state_size = w_states.shape[1] // 2
    head_size = inner_here // heads_here
    lag_rows = conv_inner.shape[0] - 1
    block_ids = jnp.arange(total_blocks, dtype=jnp.int32)
    same_owner = block_owner[:, None] == block_owner[None, :]
    first_block = jnp.min(jnp.where(same_owner, block_ids[None, :], total_blocks), axis=1)
    starting = (first_block == block_ids).astype(jnp.int32)
    request_ids = jnp.arange(lengths.shape[0], dtype=jnp.int32)
    own_length = jnp.sum(
        jnp.where(block_owner[:, None] == request_ids[None, :], lengths[None, :], 0), axis=1
    )
    valid_rows = jnp.clip(own_length - (block_ids - first_block) * BLOCK, 0, BLOCK)
    seq_index = lax.axis_index("seq")
    local_start = lax.dynamic_slice_in_dim(starting, seq_index * local_blocks, local_blocks)
    local_valid = lax.dynamic_slice_in_dim(valid_rows, seq_index * local_blocks, local_blocks)
    in_block = jnp.arange(row_count, dtype=jnp.int32) % BLOCK
    carry_on = jnp.repeat(local_start == 0, BLOCK)
    whole = lax.all_gather(tokens, "tp", axis=1, tiled=True)
    local_rows = w_inner.shape[0]
    joined = jnp.concatenate(
        [w_inner.reshape(local_rows, 2 * inner_here), w_states, w_step], axis=1
    )
    weights = lax.all_gather(joined, "seq", axis=0, tiled=True)
    all_sum = jnp.dot(whole, weights, preferred_element_type=jnp.float32)
    projected = all_sum.astype(jnp.bfloat16)
    gate_in = projected[:, :inner_here]
    x_in = projected[:, inner_here : 2 * inner_here]
    bc_in = projected[:, 2 * inner_here : 2 * inner_here + 2 * state_size]
    step_raw = projected[:, 2 * inner_here + 2 * state_size :]
    edge_inner, edge_states = passed_along(
        (x_in[row_count - lag_rows :], bc_in[row_count - lag_rows :]), "seq", 1
    )
    x_conv = convolve(x_in, edge_inner, conv_inner, in_block, carry_on)
    bc_conv = convolve(bc_in, edge_states, conv_states, in_block, carry_on)
    step_size = jax.nn.softplus(step_raw.astype(jnp.float32) + step_bias)
    log_decay = -decay_rate * step_size
    x_heads = x_conv.reshape(local_blocks, BLOCK, heads_here, head_size)
    b_rows = bc_conv[:, :state_size].reshape(local_blocks, BLOCK, state_size)
    c_rows = bc_conv[:, state_size:].reshape(local_blocks, BLOCK, state_size)
    step_blocks = step_size.reshape(local_blocks, BLOCK, heads_here)
    cumulative = jnp.cumsum(log_decay.reshape(local_blocks, BLOCK, heads_here), axis=1)
    causal = jnp.arange(BLOCK)[:, None] >= jnp.arange(BLOCK)[None, :]
    spread = cumulative[:, :, None, :] - cumulative[:, None, :, :]
    decays = jnp.exp(jnp.where(causal[None, :, :, None], spread, -jnp.inf))
    intersection = jnp.einsum("cin,cjn->cij", c_rows, b_rows, preferred_element_type=jnp.float32)
    mixing = (decays * intersection[:, :, :, None] * step_blocks[:, None, :, :]).astype(
        jnp.bfloat16
    )
    y_inner = jnp.einsum("cijh,cjhp->cihp", mixing, x_heads, preferred_element_type=jnp.float32)
    final_log = cumulative[:, -1, :]
    tail_weight = jnp.exp(final_log[:, None, :] - cumulative) * step_blocks
    weighted_b = (tail_weight[:, :, :, None] * b_rows.astype(jnp.float32)[:, :, None, :]).astype(
        jnp.bfloat16
    )
    fresh = jnp.einsum("cjhn,cjhp->chnp", weighted_b, x_heads, preferred_element_type=jnp.float32)
    keep_flag = jnp.where(local_start == 1, 0.0, 1.0).astype(jnp.float32)
    block_gain_each = jnp.exp(final_log) * keep_flag[:, None]

    def fold_block(carry, item):
        gain_now, fresh_now = item
        return ((carry[0] * gain_now, gain_now[:, None, None] * carry[1] + fresh_now), None)

    zero_state = jnp.zeros((heads_here, state_size, head_size), jnp.float32)
    unit_gain = jnp.ones((heads_here,), jnp.float32)
    (block_gain, block_state), _ = lax.scan(
        fold_block, (unit_gain, zero_state), (block_gain_each, fresh)
    )

    def packed(gain, state):
        rows = jnp.broadcast_to(gain[:, None, None], (heads_here, 1, head_size))
        return jnp.concatenate([state, rows], axis=1)

    prefix = passed_along(packed(block_gain, block_state), "seq", 1)
    reach = 1
    while reach < lax.axis_size("seq") - 1:
        earlier = passed_along(prefix, "seq", reach)
        gain_now = prefix[:, state_size:, :1]
        prefix = jnp.concatenate(
            [
                gain_now * earlier[:, :state_size] + prefix[:, :state_size],
                gain_now * earlier[:, state_size:],
            ],
            axis=1,
        )
        reach *= 2
    entering = prefix[:, :state_size]

    def pass_block(previous, item):
        log_now, keep_now, fresh_now = item
        incoming = previous * keep_now
        return (jnp.exp(log_now)[:, None, None] * incoming + fresh_now, incoming)

    _, incoming_all = lax.scan(pass_block, entering, (final_log, keep_flag, fresh))
    incoming_half = incoming_all.astype(jnp.bfloat16)
    y_carry = jnp.exp(cumulative)[:, :, :, None] * jnp.einsum(
        "cin,chnp->cihp", c_rows, incoming_half, preferred_element_type=jnp.float32
    )
    y_total = (y_inner + y_carry).reshape(row_count, inner_here) + jnp.repeat(skip_gain, head_size)[
        None, :
    ] * x_conv.astype(jnp.float32)
    gated = y_total * jax.nn.silu(gate_in.astype(jnp.float32))
    squares = lax.psum(jnp.sum(gated * gated, axis=1), "tp")
    square_mean = squares / (inner_here * lax.axis_size("tp"))
    normed = (gated * lax.rsqrt(square_mean + 1e-05)[:, None] * norm_gain).astype(jnp.bfloat16)
    partial_out = jnp.dot(
        normed,
        lax.all_gather(w_output, "seq", axis=1, tiled=True),
        preferred_element_type=jnp.float32,
    )
    summed = lax.psum_scatter(partial_out, "tp", scatter_dimension=1, tiled=True)
    live = in_block < jnp.repeat(local_valid, BLOCK)
    return jnp.where(live[:, None], summed, 0.0).astype(jnp.bfloat16)


def solution(mesh):
    return jax.shard_map(
        on_device,
        mesh=mesh,
        in_specs=(
            P("seq", "tp"),
            P("seq", None, "tp"),
            P("seq", None),
            P("seq", "tp"),
            P(None, "tp"),
            P(),
            P("tp"),
            P("tp"),
            P("tp"),
            P("tp"),
            P("tp", "seq"),
            P(),
            P(),
        ),
        out_specs=P("seq", "tp"),
        check_vma=False,
    )
```

```python
import jax
import jax.numpy as jnp
from jax import lax
from jax.sharding import Mesh
from jax.sharding import PartitionSpec as P

BLOCK = 256
LONGEST = 64
SEQ = ("sx", "sz")
SEQ_INNER = 8


def passed_along(value, axis, by):
    count = lax.axis_size(axis)
    pairs = [(i, i + by) for i in range(count) if 0 <= i + by < count]
    return lax.ppermute(value, axis, pairs)


def convolve(values, edge_rows, weights, in_block, carry_on):
    lag_rows = weights.shape[0] - 1
    row_total = values.shape[0]
    widened = jnp.concatenate([edge_rows, values], axis=0).astype(jnp.float32)
    total = jnp.zeros(values.shape, jnp.float32)
    for offset in range(weights.shape[0]):
        shifted = widened[lag_rows - offset : lag_rows - offset + row_total]
        keeping = (in_block >= offset) | carry_on
        total = total + jnp.where(keeping[:, None], shifted, 0.0) * weights[offset]
    return jax.nn.silu(total).astype(jnp.bfloat16)


def on_device(
    tokens,
    w_inner,
    w_states,
    w_step,
    conv_inner,
    conv_states,
    decay_rate,
    step_bias,
    skip_gain,
    norm_gain,
    w_output,
    block_owner,
    lengths,
):
    row_count = tokens.shape[0]
    local_blocks = row_count // BLOCK
    total_blocks = block_owner.shape[0]
    heads_here = w_step.shape[1]
    inner_here = w_inner.shape[2]
    state_size = w_states.shape[1] // 2
    head_size = inner_here // heads_here
    lag_rows = conv_inner.shape[0] - 1
    block_ids = jnp.arange(total_blocks, dtype=jnp.int32)
    same_owner = block_owner[:, None] == block_owner[None, :]
    first_block = jnp.min(jnp.where(same_owner, block_ids[None, :], total_blocks), axis=1)
    starting = (first_block == block_ids).astype(jnp.int32)
    request_ids = jnp.arange(lengths.shape[0], dtype=jnp.int32)
    own_length = jnp.sum(
        jnp.where(block_owner[:, None] == request_ids[None, :], lengths[None, :], 0), axis=1
    )
    valid_rows = jnp.clip(own_length - (block_ids - first_block) * BLOCK, 0, BLOCK)
    seq_index = lax.axis_index(SEQ)
    local_start = lax.dynamic_slice_in_dim(starting, seq_index * local_blocks, local_blocks)
    local_valid = lax.dynamic_slice_in_dim(valid_rows, seq_index * local_blocks, local_blocks)
    in_block = jnp.arange(row_count, dtype=jnp.int32) % BLOCK
    carry_on = jnp.repeat(local_start == 0, BLOCK)
    whole = lax.all_gather(tokens, "tp", axis=1, tiled=True)
    local_rows = w_inner.shape[0]
    joined = jnp.concatenate(
        [w_inner.reshape(local_rows, 2 * inner_here), w_states, w_step], axis=1
    )
    weights = lax.all_gather(
        lax.all_gather(joined, "sz", axis=0, tiled=True), "sx", axis=0, tiled=True
    )
    all_sum = jnp.dot(whole, weights, preferred_element_type=jnp.float32)
    projected = all_sum.astype(jnp.bfloat16)
    gate_in = projected[:, :inner_here]
    x_in = projected[:, inner_here : 2 * inner_here]
    bc_in = projected[:, 2 * inner_here : 2 * inner_here + 2 * state_size]
    step_raw = projected[:, 2 * inner_here + 2 * state_size :]
    edge_inner, edge_states = passed_along(
        (x_in[row_count - lag_rows :], bc_in[row_count - lag_rows :]), SEQ, 1
    )
    x_conv = convolve(x_in, edge_inner, conv_inner, in_block, carry_on)
    bc_conv = convolve(bc_in, edge_states, conv_states, in_block, carry_on)
    step_size = jax.nn.softplus(step_raw.astype(jnp.float32) + step_bias)
    log_decay = -decay_rate * step_size
    x_heads = x_conv.reshape(local_blocks, BLOCK, heads_here, head_size)
    b_rows = bc_conv[:, :state_size].reshape(local_blocks, BLOCK, state_size)
    c_rows = bc_conv[:, state_size:].reshape(local_blocks, BLOCK, state_size)
    step_blocks = step_size.reshape(local_blocks, BLOCK, heads_here)
    cumulative = jnp.cumsum(log_decay.reshape(local_blocks, BLOCK, heads_here), axis=1)
    causal = jnp.arange(BLOCK)[:, None] >= jnp.arange(BLOCK)[None, :]
    spread = cumulative[:, :, None, :] - cumulative[:, None, :, :]
    decays = jnp.exp(jnp.where(causal[None, :, :, None], spread, -jnp.inf))
    intersection = jnp.einsum("cin,cjn->cij", c_rows, b_rows, preferred_element_type=jnp.float32)
    mixing = (decays * intersection[:, :, :, None] * step_blocks[:, None, :, :]).astype(
        jnp.bfloat16
    )
    y_inner = jnp.einsum("cijh,cjhp->cihp", mixing, x_heads, preferred_element_type=jnp.float32)
    final_log = cumulative[:, -1, :]
    tail_weight = jnp.exp(final_log[:, None, :] - cumulative) * step_blocks
    weighted_b = (tail_weight[:, :, :, None] * b_rows.astype(jnp.float32)[:, :, None, :]).astype(
        jnp.bfloat16
    )
    fresh = jnp.einsum("cjhn,cjhp->chnp", weighted_b, x_heads, preferred_element_type=jnp.float32)
    keep_flag = jnp.where(local_start == 1, 0.0, 1.0).astype(jnp.float32)
    block_gain_each = jnp.exp(final_log) * keep_flag[:, None]

    def fold_block(carry, item):
        gain_now, fresh_now = item
        return ((carry[0] * gain_now, gain_now[:, None, None] * carry[1] + fresh_now), None)

    zero_state = jnp.zeros((heads_here, state_size, head_size), jnp.float32)
    unit_gain = jnp.ones((heads_here,), jnp.float32)
    (block_gain, block_state), _ = lax.scan(
        fold_block, (unit_gain, zero_state), (block_gain_each, fresh)
    )

    def packed(gain, state):
        rows = jnp.broadcast_to(gain[:, None, None], (heads_here, 1, head_size))
        return jnp.concatenate([state, rows], axis=1)

    prefix = passed_along(packed(block_gain, block_state), SEQ, 1)
    needed = min(-(-(LONGEST - 1) // local_blocks), lax.axis_size(SEQ) - 1)
    reach = 1
    while reach < needed:
        earlier = passed_along(prefix, SEQ, reach)
        gain_now = prefix[:, state_size:, :1]
        prefix = jnp.concatenate(
            [
                gain_now * earlier[:, :state_size] + prefix[:, :state_size],
                gain_now * earlier[:, state_size:],
            ],
            axis=1,
        )
        reach *= 2
    entering = prefix[:, :state_size]

    def pass_block(previous, item):
        log_now, keep_now, fresh_now = item
        incoming = previous * keep_now
        return (jnp.exp(log_now)[:, None, None] * incoming + fresh_now, incoming)

    _, incoming_all = lax.scan(pass_block, entering, (final_log, keep_flag, fresh))
    incoming_half = incoming_all.astype(jnp.bfloat16)
    y_carry = jnp.exp(cumulative)[:, :, :, None] * jnp.einsum(
        "cin,chnp->cihp", c_rows, incoming_half, preferred_element_type=jnp.float32
    )
    y_total = (y_inner + y_carry).reshape(row_count, inner_here) + jnp.repeat(skip_gain, head_size)[
        None, :
    ] * x_conv.astype(jnp.float32)
    gated = y_total * jax.nn.silu(gate_in.astype(jnp.float32))
    squares = lax.psum(jnp.sum(gated * gated, axis=1), "tp")
    square_mean = squares / (inner_here * lax.axis_size("tp"))
    normed = (gated * lax.rsqrt(square_mean + 1e-05)[:, None] * norm_gain).astype(jnp.bfloat16)
    partial_out = jnp.dot(
        normed,
        lax.all_gather(
            lax.all_gather(w_output, "sz", axis=1, tiled=True), "sx", axis=1, tiled=True
        ),
        preferred_element_type=jnp.float32,
    )
    summed = lax.psum_scatter(partial_out, "tp", scatter_dimension=1, tiled=True)
    live = in_block < jnp.repeat(local_valid, BLOCK)
    return jnp.where(live[:, None], summed, 0.0).astype(jnp.bfloat16)


def solution(mesh):
    seq_count, tp_count = mesh.devices.shape
    split = Mesh(
        mesh.devices.reshape(seq_count // SEQ_INNER, SEQ_INNER, tp_count), ("sx", "sz", "tp")
    )
    return jax.shard_map(
        on_device,
        mesh=split,
        in_specs=(
            P(SEQ, "tp"),
            P(SEQ, None, "tp"),
            P(SEQ, None),
            P(SEQ, "tp"),
            P(None, "tp"),
            P(),
            P("tp"),
            P("tp"),
            P("tp"),
            P("tp"),
            P("tp", SEQ),
            P(),
            P(),
        ),
        out_specs=P(SEQ, "tp"),
        check_vma=False,
    )
```

```python
import jax
import jax.numpy as jnp
from jax import lax
from jax.sharding import PartitionSpec as P

BLOCK = 256
LONGEST = 64


def passed_along(value, axis, by):
    count = lax.axis_size(axis)
    pairs = [(i, i + by) for i in range(count) if 0 <= i + by < count]
    return lax.ppermute(value, axis, pairs)


def convolve(values, edge_rows, weights, in_block, carry_on):
    lag_rows = weights.shape[0] - 1
    row_total = values.shape[0]
    widened = jnp.concatenate([edge_rows, values], axis=0).astype(jnp.float32)
    total = jnp.zeros(values.shape, jnp.float32)
    for offset in range(weights.shape[0]):
        shifted = widened[lag_rows - offset : lag_rows - offset + row_total]
        keeping = (in_block >= offset) | carry_on
        total = total + jnp.where(keeping[:, None], shifted, 0.0) * weights[offset]
    return jax.nn.silu(total).astype(jnp.bfloat16)


def on_device(
    tokens,
    w_inner,
    w_states,
    w_step,
    conv_inner,
    conv_states,
    decay_rate,
    step_bias,
    skip_gain,
    norm_gain,
    w_output,
    block_owner,
    lengths,
):
    row_count = tokens.shape[0]
    local_blocks = row_count // BLOCK
    total_blocks = block_owner.shape[0]
    heads_here = w_step.shape[1]
    inner_here = w_inner.shape[2]
    state_size = w_states.shape[1] // 2
    head_size = inner_here // heads_here
    lag_rows = conv_inner.shape[0] - 1
    block_ids = jnp.arange(total_blocks, dtype=jnp.int32)
    same_owner = block_owner[:, None] == block_owner[None, :]
    first_block = jnp.min(jnp.where(same_owner, block_ids[None, :], total_blocks), axis=1)
    starting = (first_block == block_ids).astype(jnp.int32)
    request_ids = jnp.arange(lengths.shape[0], dtype=jnp.int32)
    own_length = jnp.sum(
        jnp.where(block_owner[:, None] == request_ids[None, :], lengths[None, :], 0), axis=1
    )
    valid_rows = jnp.clip(own_length - (block_ids - first_block) * BLOCK, 0, BLOCK)
    seq_index = lax.axis_index("seq")
    local_start = lax.dynamic_slice_in_dim(starting, seq_index * local_blocks, local_blocks)
    local_valid = lax.dynamic_slice_in_dim(valid_rows, seq_index * local_blocks, local_blocks)
    in_block = jnp.arange(row_count, dtype=jnp.int32) % BLOCK
    carry_on = jnp.repeat(local_start == 0, BLOCK)
    whole = lax.all_gather(tokens, "tp", axis=1, tiled=True)
    first_cols = jnp.concatenate([w_inner[:, 1, :], w_states, w_step], axis=1)
    first_weights = lax.all_gather(first_cols, "seq", axis=0, tiled=True)
    gate_weights = lax.all_gather(w_inner[:, 0, :], "seq", axis=0, tiled=True)
    first_sum = jnp.dot(whole, first_weights, preferred_element_type=jnp.float32)
    projected = first_sum.astype(jnp.bfloat16)
    x_in = projected[:, :inner_here]
    bc_in = projected[:, inner_here : inner_here + 2 * state_size]
    step_raw = projected[:, inner_here + 2 * state_size :]
    gate_in = jnp.dot(whole, gate_weights, preferred_element_type=jnp.float32).astype(jnp.bfloat16)
    edge_inner, edge_states = passed_along(
        (x_in[row_count - lag_rows :], bc_in[row_count - lag_rows :]), "seq", 1
    )
    x_conv = convolve(x_in, edge_inner, conv_inner, in_block, carry_on)
    bc_conv = convolve(bc_in, edge_states, conv_states, in_block, carry_on)
    step_size = jax.nn.softplus(step_raw.astype(jnp.float32) + step_bias)
    log_decay = -decay_rate * step_size
    x_heads = x_conv.reshape(local_blocks, BLOCK, heads_here, head_size)
    b_rows = bc_conv[:, :state_size].reshape(local_blocks, BLOCK, state_size)
    c_rows = bc_conv[:, state_size:].reshape(local_blocks, BLOCK, state_size)
    step_blocks = step_size.reshape(local_blocks, BLOCK, heads_here)
    cumulative = jnp.cumsum(log_decay.reshape(local_blocks, BLOCK, heads_here), axis=1)
    causal = jnp.arange(BLOCK)[:, None] >= jnp.arange(BLOCK)[None, :]
    spread = cumulative[:, :, None, :] - cumulative[:, None, :, :]
    decays = jnp.exp(jnp.where(causal[None, :, :, None], spread, -jnp.inf))
    intersection = jnp.einsum("cin,cjn->cij", c_rows, b_rows, preferred_element_type=jnp.float32)
    mixing = (decays * intersection[:, :, :, None] * step_blocks[:, None, :, :]).astype(
        jnp.bfloat16
    )
    y_inner = jnp.einsum("cijh,cjhp->cihp", mixing, x_heads, preferred_element_type=jnp.float32)
    final_log = cumulative[:, -1, :]
    tail_weight = jnp.exp(final_log[:, None, :] - cumulative) * step_blocks
    weighted_b = (tail_weight[:, :, :, None] * b_rows.astype(jnp.float32)[:, :, None, :]).astype(
        jnp.bfloat16
    )
    fresh = jnp.einsum("cjhn,cjhp->chnp", weighted_b, x_heads, preferred_element_type=jnp.float32)
    keep_flag = jnp.where(local_start == 1, 0.0, 1.0).astype(jnp.float32)
    block_gain_each = jnp.exp(final_log) * keep_flag[:, None]

    block_gain = jnp.ones((heads_here,), jnp.float32)
    block_state = jnp.zeros((heads_here, state_size, head_size), jnp.float32)
    gains_in, states_in = [], []
    for block in range(local_blocks):
        gains_in.append(block_gain * keep_flag[block])
        states_in.append(block_state * keep_flag[block])
        block_gain = block_gain * block_gain_each[block]
        block_state = block_gain_each[block][:, None, None] * block_state + fresh[block]

    def packed(gain, state):
        rows = jnp.broadcast_to(gain[:, None, None], (heads_here, 1, head_size))
        return jnp.concatenate([state, rows], axis=1)

    prefix = passed_along(packed(block_gain, block_state), "seq", 1)
    needed = min(-(-(LONGEST - 1) // local_blocks), lax.axis_size("seq") - 1)
    reach = 1
    while reach < needed:
        earlier = passed_along(prefix, "seq", reach)
        gain_now = prefix[:, state_size:, :1]
        prefix = jnp.concatenate(
            [
                gain_now * earlier[:, :state_size] + prefix[:, :state_size],
                gain_now * earlier[:, state_size:],
            ],
            axis=1,
        )
        reach *= 2
    entering = prefix[:, :state_size]
    incoming_all = (
        jnp.stack(gains_in)[:, :, None, None] * entering[None] + jnp.stack(states_in)
    )
    incoming_half = incoming_all.astype(jnp.bfloat16)
    y_carry = jnp.exp(cumulative)[:, :, :, None] * jnp.einsum(
        "cin,chnp->cihp", c_rows, incoming_half, preferred_element_type=jnp.float32
    )
    y_total = (y_inner + y_carry).reshape(row_count, inner_here) + jnp.repeat(skip_gain, head_size)[
        None, :
    ] * x_conv.astype(jnp.float32)
    gated = y_total * jax.nn.silu(gate_in.astype(jnp.float32))
    squares = jnp.sum(gated * gated, axis=1)
    scaled = (gated * norm_gain).astype(jnp.bfloat16)
    partial_out = jnp.dot(
        scaled,
        lax.all_gather(w_output, "seq", axis=1, tiled=True),
        preferred_element_type=jnp.float32,
    )
    tp_count = lax.axis_size("tp")
    cols_here = partial_out.shape[1] // tp_count
    square_rows = jnp.tile(squares.reshape(row_count // cols_here, cols_here), (1, tp_count))
    summed = lax.psum_scatter(
        jnp.concatenate([partial_out, square_rows], axis=0), "tp", scatter_dimension=1, tiled=True
    )
    square_mean = summed[row_count:].reshape(row_count) / (inner_here * tp_count)
    mixed = summed[:row_count] * lax.rsqrt(square_mean + 1e-05)[:, None]
    live = in_block < jnp.repeat(local_valid, BLOCK)
    return jnp.where(live[:, None], mixed, 0.0).astype(jnp.bfloat16)


def solution(mesh):
    return jax.shard_map(
        on_device,
        mesh=mesh,
        in_specs=(
            P("seq", "tp"),
            P("seq", None, "tp"),
            P("seq", None),
            P("seq", "tp"),
            P(None, "tp"),
            P(),
            P("tp"),
            P("tp"),
            P("tp"),
            P("tp"),
            P("tp", "seq"),
            P(),
            P(),
        ),
        out_specs=P("seq", "tp"),
        check_vma=False,
    )
```

```python
import jax
import jax.numpy as jnp
from jax import lax
from jax.sharding import PartitionSpec as P

BLOCK = 256
LONGEST = 64


def passed_along(value, axis, by):
    count = lax.axis_size(axis)
    pairs = [(i, i + by) for i in range(count) if 0 <= i + by < count]
    return lax.ppermute(value, axis, pairs)


def convolve(values, edge_rows, weights, in_block, carry_on):
    lag_rows = weights.shape[0] - 1
    row_total = values.shape[0]
    widened = jnp.concatenate([edge_rows, values], axis=0).astype(jnp.float32)
    total = jnp.zeros(values.shape, jnp.float32)
    for offset in range(weights.shape[0]):
        shifted = widened[lag_rows - offset : lag_rows - offset + row_total]
        keeping = (in_block >= offset) | carry_on
        total = total + jnp.where(keeping[:, None], shifted, 0.0) * weights[offset]
    return jax.nn.silu(total).astype(jnp.bfloat16)


def on_device(
    tokens,
    w_inner,
    w_states,
    w_step,
    conv_inner,
    conv_states,
    decay_rate,
    step_bias,
    skip_gain,
    norm_gain,
    w_output,
    block_owner,
    lengths,
):
    row_count = tokens.shape[0]
    local_blocks = row_count // BLOCK
    total_blocks = block_owner.shape[0]
    heads_here = w_step.shape[1]
    inner_here = w_inner.shape[2]
    state_size = w_states.shape[1] // 2
    head_size = inner_here // heads_here
    lag_rows = conv_inner.shape[0] - 1
    block_ids = jnp.arange(total_blocks, dtype=jnp.int32)
    same_owner = block_owner[:, None] == block_owner[None, :]
    first_block = jnp.min(jnp.where(same_owner, block_ids[None, :], total_blocks), axis=1)
    starting = (first_block == block_ids).astype(jnp.int32)
    request_ids = jnp.arange(lengths.shape[0], dtype=jnp.int32)
    own_length = jnp.sum(
        jnp.where(block_owner[:, None] == request_ids[None, :], lengths[None, :], 0), axis=1
    )
    valid_rows = jnp.clip(own_length - (block_ids - first_block) * BLOCK, 0, BLOCK)
    seq_index = lax.axis_index("seq")
    local_start = lax.dynamic_slice_in_dim(starting, seq_index * local_blocks, local_blocks)
    local_valid = lax.dynamic_slice_in_dim(valid_rows, seq_index * local_blocks, local_blocks)
    in_block = jnp.arange(row_count, dtype=jnp.int32) % BLOCK
    carry_on = jnp.repeat(local_start == 0, BLOCK)
    tp_count = lax.axis_size("tp")
    tp_index = lax.axis_index("tp")
    token_cols = tokens.shape[1]
    whole = jnp.zeros((row_count, token_cols * tp_count), tokens.dtype)
    whole = lax.dynamic_update_slice_in_dim(whole, tokens, tp_index * token_cols, axis=1)
    for shift in range(1, tp_count):
        arrived = lax.ppermute(
            tokens, "tp", [(i, (i + shift) % tp_count) for i in range(tp_count)]
        )
        origin = (tp_index + tp_count - shift) % tp_count
        whole = lax.dynamic_update_slice_in_dim(whole, arrived, origin * token_cols, axis=1)
    first_cols = jnp.concatenate([w_inner[:, 1, :], w_states, w_step], axis=1)
    first_weights = lax.all_gather(first_cols, "seq", axis=0, tiled=True)
    late_cols = jnp.concatenate([w_inner[:, 0, :], w_output.T], axis=1)
    late_weights = lax.all_gather(late_cols, "seq", axis=0, tiled=True)
    gate_weights = late_weights[:, :inner_here]
    out_weights = late_weights[:, inner_here:]
    first_sum = jnp.dot(whole, first_weights, preferred_element_type=jnp.float32)
    projected = first_sum.astype(jnp.bfloat16)
    x_in = projected[:, :inner_here]
    bc_in = projected[:, inner_here : inner_here + 2 * state_size]
    step_raw = projected[:, inner_here + 2 * state_size :]
    gate_in = jnp.dot(whole, gate_weights, preferred_element_type=jnp.float32).astype(jnp.bfloat16)
    edge_inner, edge_states = passed_along(
        (x_in[row_count - lag_rows :], bc_in[row_count - lag_rows :]), "seq", 1
    )
    x_conv = convolve(x_in, edge_inner, conv_inner, in_block, carry_on)
    bc_conv = convolve(bc_in, edge_states, conv_states, in_block, carry_on)
    step_size = jax.nn.softplus(step_raw.astype(jnp.float32) + step_bias)
    log_decay = -decay_rate * step_size
    x_heads = x_conv.reshape(local_blocks, BLOCK, heads_here, head_size)
    b_rows = bc_conv[:, :state_size].reshape(local_blocks, BLOCK, state_size)
    c_rows = bc_conv[:, state_size:].reshape(local_blocks, BLOCK, state_size)
    step_blocks = step_size.reshape(local_blocks, BLOCK, heads_here)
    cumulative = jnp.cumsum(log_decay.reshape(local_blocks, BLOCK, heads_here), axis=1)
    causal = jnp.arange(BLOCK)[:, None] >= jnp.arange(BLOCK)[None, :]
    spread = cumulative[:, :, None, :] - cumulative[:, None, :, :]
    decays = jnp.exp(jnp.where(causal[None, :, :, None], spread, -jnp.inf))
    intersection = jnp.einsum("cin,cjn->cij", c_rows, b_rows, preferred_element_type=jnp.float32)
    mixing = (decays * intersection[:, :, :, None] * step_blocks[:, None, :, :]).astype(
        jnp.bfloat16
    )
    y_inner = jnp.einsum("cijh,cjhp->cihp", mixing, x_heads, preferred_element_type=jnp.float32)
    final_log = cumulative[:, -1, :]
    tail_weight = jnp.exp(final_log[:, None, :] - cumulative) * step_blocks
    weighted_b = (tail_weight[:, :, :, None] * b_rows.astype(jnp.float32)[:, :, None, :]).astype(
        jnp.bfloat16
    )
    fresh = jnp.einsum("cjhn,cjhp->chnp", weighted_b, x_heads, preferred_element_type=jnp.float32)
    keep_flag = jnp.where(local_start == 1, 0.0, 1.0).astype(jnp.float32)
    block_gain_each = jnp.exp(final_log) * keep_flag[:, None]

    block_gain = jnp.ones((heads_here,), jnp.float32)
    block_state = jnp.zeros((heads_here, state_size, head_size), jnp.float32)
    gains_in, states_in = [], []
    for block in range(local_blocks):
        gains_in.append(block_gain * keep_flag[block])
        states_in.append(block_state * keep_flag[block])
        block_gain = block_gain * block_gain_each[block]
        block_state = block_gain_each[block][:, None, None] * block_state + fresh[block]

    def packed(gain, state):
        rows = jnp.broadcast_to(gain[:, None, None], (heads_here, 1, head_size))
        return jnp.concatenate([state, rows], axis=1)

    prefix = passed_along(packed(block_gain, block_state), "seq", 1)
    needed = min(-(-(LONGEST - 1) // local_blocks), lax.axis_size("seq") - 1)
    reach = 1
    while reach < needed:
        earlier = passed_along(prefix, "seq", reach)
        gain_now = prefix[:, state_size:, :1]
        prefix = jnp.concatenate(
            [
                gain_now * earlier[:, :state_size] + prefix[:, :state_size],
                gain_now * earlier[:, state_size:],
            ],
            axis=1,
        )
        reach *= 2
    entering = prefix[:, :state_size]
    incoming_all = (
        jnp.stack(gains_in)[:, :, None, None] * entering[None] + jnp.stack(states_in)
    )
    incoming_half = incoming_all.astype(jnp.bfloat16)
    y_carry = jnp.exp(cumulative)[:, :, :, None] * jnp.einsum(
        "cin,chnp->cihp", c_rows, incoming_half, preferred_element_type=jnp.float32
    )
    y_total = (y_inner + y_carry).reshape(row_count, inner_here) + jnp.repeat(skip_gain, head_size)[
        None, :
    ] * x_conv.astype(jnp.float32)
    gated = y_total * jax.nn.silu(gate_in.astype(jnp.float32))
    squares = jnp.sum(gated * gated, axis=1)
    scaled = (gated * norm_gain).astype(jnp.bfloat16)
    partial_out = lax.dot_general(
        scaled, out_weights, (((1,), (1,)), ((), ())), preferred_element_type=jnp.float32
    )
    cols_here = partial_out.shape[1] // tp_count
    square_rows = jnp.tile(squares.reshape(row_count // cols_here, cols_here), (1, tp_count))
    summed = lax.psum_scatter(
        jnp.concatenate([partial_out, square_rows], axis=0), "tp", scatter_dimension=1, tiled=True
    )
    square_mean = summed[row_count:].reshape(row_count) / (inner_here * tp_count)
    mixed = summed[:row_count] * lax.rsqrt(square_mean + 1e-05)[:, None]
    live = in_block < jnp.repeat(local_valid, BLOCK)
    return jnp.where(live[:, None], mixed, 0.0).astype(jnp.bfloat16)


def solution(mesh):
    return jax.shard_map(
        on_device,
        mesh=mesh,
        in_specs=(
            P("seq", "tp"),
            P("seq", None, "tp"),
            P("seq", None),
            P("seq", "tp"),
            P(None, "tp"),
            P(),
            P("tp"),
            P("tp"),
            P("tp"),
            P("tp"),
            P("tp", "seq"),
            P(),
            P(),
        ),
        out_specs=P("seq", "tp"),
        check_vma=False,
    )
```

```python
import jax
import jax.numpy as jnp
from jax import lax
from jax.sharding import PartitionSpec as P

BLOCK = 256
LONGEST = 64
RADIX = 4


def passed_along(value, axis, by):
    count = lax.axis_size(axis)
    pairs = [(i, i + by) for i in range(count) if 0 <= i + by < count]
    return lax.ppermute(value, axis, pairs)


def convolve(values, edge_rows, weights, in_block, carry_on):
    lag_rows = weights.shape[0] - 1
    row_total = values.shape[0]
    widened = jnp.concatenate([edge_rows, values], axis=0).astype(jnp.float32)
    total = jnp.zeros(values.shape, jnp.float32)
    for offset in range(weights.shape[0]):
        shifted = widened[lag_rows - offset : lag_rows - offset + row_total]
        keeping = (in_block >= offset) | carry_on
        total = total + jnp.where(keeping[:, None], shifted, 0.0) * weights[offset]
    return jax.nn.silu(total).astype(jnp.bfloat16)


def on_device(
    tokens,
    w_inner,
    w_states,
    w_step,
    conv_inner,
    conv_states,
    decay_rate,
    step_bias,
    skip_gain,
    norm_gain,
    w_output,
    block_owner,
    lengths,
):
    row_count = tokens.shape[0]
    local_blocks = row_count // BLOCK
    total_blocks = block_owner.shape[0]
    heads_here = w_step.shape[1]
    inner_here = w_inner.shape[2]
    state_size = w_states.shape[1] // 2
    head_size = inner_here // heads_here
    lag_rows = conv_inner.shape[0] - 1
    block_ids = jnp.arange(total_blocks, dtype=jnp.int32)
    same_owner = block_owner[:, None] == block_owner[None, :]
    first_block = jnp.min(jnp.where(same_owner, block_ids[None, :], total_blocks), axis=1)
    starting = (first_block == block_ids).astype(jnp.int32)
    request_ids = jnp.arange(lengths.shape[0], dtype=jnp.int32)
    own_length = jnp.sum(
        jnp.where(block_owner[:, None] == request_ids[None, :], lengths[None, :], 0), axis=1
    )
    valid_rows = jnp.clip(own_length - (block_ids - first_block) * BLOCK, 0, BLOCK)
    seq_index = lax.axis_index("seq")
    local_start = lax.dynamic_slice_in_dim(starting, seq_index * local_blocks, local_blocks)
    local_valid = lax.dynamic_slice_in_dim(valid_rows, seq_index * local_blocks, local_blocks)
    in_block = jnp.arange(row_count, dtype=jnp.int32) % BLOCK
    carry_on = jnp.repeat(local_start == 0, BLOCK)
    tp_count = lax.axis_size("tp")
    tp_index = lax.axis_index("tp")
    token_cols = tokens.shape[1]
    whole = jnp.zeros((row_count, token_cols * tp_count), tokens.dtype)
    whole = lax.dynamic_update_slice_in_dim(whole, tokens, tp_index * token_cols, axis=1)
    for shift in range(1, tp_count):
        arrived = lax.ppermute(
            tokens, "tp", [(i, (i + shift) % tp_count) for i in range(tp_count)]
        )
        origin = (tp_index + tp_count - shift) % tp_count
        whole = lax.dynamic_update_slice_in_dim(whole, arrived, origin * token_cols, axis=1)
    first_cols = jnp.concatenate([w_inner[:, 1, :], w_states, w_step], axis=1)
    first_weights = lax.all_gather(first_cols, "seq", axis=0, tiled=True)
    late_cols = jnp.concatenate([w_inner[:, 0, :], w_output.T], axis=1)
    late_weights = lax.all_gather(late_cols, "seq", axis=0, tiled=True)
    gate_weights = late_weights[:, :inner_here]
    out_weights = late_weights[:, inner_here:]
    first_sum = jnp.dot(whole, first_weights, preferred_element_type=jnp.float32)
    projected = first_sum.astype(jnp.bfloat16)
    x_in = projected[:, :inner_here]
    bc_in = projected[:, inner_here : inner_here + 2 * state_size]
    step_raw = projected[:, inner_here + 2 * state_size :]
    gate_in = jnp.dot(whole, gate_weights, preferred_element_type=jnp.float32).astype(jnp.bfloat16)
    edge_inner, edge_states = passed_along(
        (x_in[row_count - lag_rows :], bc_in[row_count - lag_rows :]), "seq", 1
    )
    x_conv = convolve(x_in, edge_inner, conv_inner, in_block, carry_on)
    bc_conv = convolve(bc_in, edge_states, conv_states, in_block, carry_on)
    step_size = jax.nn.softplus(step_raw.astype(jnp.float32) + step_bias)
    log_decay = -decay_rate * step_size
    x_heads = x_conv.reshape(local_blocks, BLOCK, heads_here, head_size)
    b_rows = bc_conv[:, :state_size].reshape(local_blocks, BLOCK, state_size)
    c_rows = bc_conv[:, state_size:].reshape(local_blocks, BLOCK, state_size)
    step_blocks = step_size.reshape(local_blocks, BLOCK, heads_here)
    cumulative = jnp.cumsum(log_decay.reshape(local_blocks, BLOCK, heads_here), axis=1)
    causal = jnp.arange(BLOCK)[:, None] >= jnp.arange(BLOCK)[None, :]
    spread = cumulative[:, :, None, :] - cumulative[:, None, :, :]
    decays = jnp.exp(jnp.where(causal[None, :, :, None], spread, -jnp.inf))
    intersection = jnp.einsum("cin,cjn->cij", c_rows, b_rows, preferred_element_type=jnp.float32)
    mixing = (decays * intersection[:, :, :, None] * step_blocks[:, None, :, :]).astype(
        jnp.bfloat16
    )
    y_inner = jnp.einsum("cijh,cjhp->cihp", mixing, x_heads, preferred_element_type=jnp.float32)
    final_log = cumulative[:, -1, :]
    tail_weight = jnp.exp(final_log[:, None, :] - cumulative) * step_blocks
    weighted_b = (tail_weight[:, :, :, None] * b_rows.astype(jnp.float32)[:, :, None, :]).astype(
        jnp.bfloat16
    )
    fresh = jnp.einsum("cjhn,cjhp->chnp", weighted_b, x_heads, preferred_element_type=jnp.float32)
    keep_flag = jnp.where(local_start == 1, 0.0, 1.0).astype(jnp.float32)
    block_gain_each = jnp.exp(final_log) * keep_flag[:, None]

    block_gain = jnp.ones((heads_here,), jnp.float32)
    block_state = jnp.zeros((heads_here, state_size, head_size), jnp.float32)
    gains_in, states_in = [], []
    for block in range(local_blocks):
        gains_in.append(block_gain * keep_flag[block])
        states_in.append(block_state * keep_flag[block])
        block_gain = block_gain * block_gain_each[block]
        block_state = block_gain_each[block][:, None, None] * block_state + fresh[block]

    def packed(gain, state):
        rows = jnp.broadcast_to(gain[:, None, None], (heads_here, 1, head_size))
        return jnp.concatenate([state, rows], axis=1)

    def composed(later, earlier):
        gain_now = later[:, state_size:, :1]
        return jnp.concatenate(
            [
                gain_now * earlier[:, :state_size] + later[:, :state_size],
                gain_now * earlier[:, state_size:],
            ],
            axis=1,
        )

    own = packed(block_gain, block_state)
    needed = min(-(-(LONGEST - 1) // local_blocks), lax.axis_size("seq") - 1)
    arrivals = [passed_along(own, "seq", by) for by in range(1, RADIX + 1)]
    prefix = arrivals[0]
    for earlier in arrivals[1:]:
        prefix = composed(prefix, earlier)
    reach = RADIX
    while reach < needed:
        arrivals = [passed_along(prefix, "seq", reach * k) for k in range(1, RADIX)]
        for earlier in arrivals:
            prefix = composed(prefix, earlier)
        reach *= RADIX
    entering = prefix[:, :state_size]
    incoming_all = (
        jnp.stack(gains_in)[:, :, None, None] * entering[None] + jnp.stack(states_in)
    )
    incoming_half = incoming_all.astype(jnp.bfloat16)
    y_carry = jnp.exp(cumulative)[:, :, :, None] * jnp.einsum(
        "cin,chnp->cihp", c_rows, incoming_half, preferred_element_type=jnp.float32
    )
    y_total = (y_inner + y_carry).reshape(row_count, inner_here) + jnp.repeat(skip_gain, head_size)[
        None, :
    ] * x_conv.astype(jnp.float32)
    gated = y_total * jax.nn.silu(gate_in.astype(jnp.float32))
    squares = jnp.sum(gated * gated, axis=1)
    scaled = (gated * norm_gain).astype(jnp.bfloat16)
    partial_out = lax.dot_general(
        scaled, out_weights, (((1,), (1,)), ((), ())), preferred_element_type=jnp.float32
    )
    cols_here = partial_out.shape[1] // tp_count
    square_rows = jnp.tile(squares.reshape(row_count // cols_here, cols_here), (1, tp_count))
    summed = lax.psum_scatter(
        jnp.concatenate([partial_out, square_rows], axis=0), "tp", scatter_dimension=1, tiled=True
    )
    square_mean = summed[row_count:].reshape(row_count) / (inner_here * tp_count)
    mixed = summed[:row_count] * lax.rsqrt(square_mean + 1e-05)[:, None]
    live = in_block < jnp.repeat(local_valid, BLOCK)
    return jnp.where(live[:, None], mixed, 0.0).astype(jnp.bfloat16)


def solution(mesh):
    return jax.shard_map(
        on_device,
        mesh=mesh,
        in_specs=(
            P("seq", "tp"),
            P("seq", None, "tp"),
            P("seq", None),
            P("seq", "tp"),
            P(None, "tp"),
            P(),
            P("tp"),
            P("tp"),
            P("tp"),
            P("tp"),
            P("tp", "seq"),
            P(),
            P(),
        ),
        out_specs=P("seq", "tp"),
        check_vma=False,
    )
```

```python
import jax
import jax.numpy as jnp
from jax import lax
from jax.sharding import Mesh
from jax.sharding import PartitionSpec as P

BLOCK = 256
LONGEST = 64
SEQ = ("sx", "sz")
SEQ_INNER = 8


def passed_along(value, axis, by):
    count = lax.axis_size(axis)
    pairs = [(i, i + by) for i in range(count) if 0 <= i + by < count]
    return lax.ppermute(value, axis, pairs)


def gathered(value, axis, dim):
    count = lax.axis_size(axis)
    index = lax.axis_index(axis)
    size = value.shape[dim]
    shape = list(value.shape)
    shape[dim] = size * count
    out = jnp.zeros(shape, value.dtype)
    out = lax.dynamic_update_slice_in_dim(out, value, index * size, axis=dim)
    for shift in range(1, count):
        arrived = lax.ppermute(value, axis, [(i, (i + shift) % count) for i in range(count)])
        origin = (index + count - shift) % count
        out = lax.dynamic_update_slice_in_dim(out, arrived, origin * size, axis=dim)
    return out


def convolve(values, edge_rows, weights, in_block, carry_on):
    lag_rows = weights.shape[0] - 1
    row_total = values.shape[0]
    widened = jnp.concatenate([edge_rows, values], axis=0).astype(jnp.float32)
    total = jnp.zeros(values.shape, jnp.float32)
    for offset in range(weights.shape[0]):
        shifted = widened[lag_rows - offset : lag_rows - offset + row_total]
        keeping = (in_block >= offset) | carry_on
        total = total + jnp.where(keeping[:, None], shifted, 0.0) * weights[offset]
    return jax.nn.silu(total).astype(jnp.bfloat16)


def on_device(
    tokens,
    w_inner,
    w_states,
    w_step,
    conv_inner,
    conv_states,
    decay_rate,
    step_bias,
    skip_gain,
    norm_gain,
    w_output,
    block_owner,
    lengths,
):
    row_count = tokens.shape[0]
    local_blocks = row_count // BLOCK
    total_blocks = block_owner.shape[0]
    heads_here = w_step.shape[1]
    inner_here = w_inner.shape[2]
    state_size = w_states.shape[1] // 2
    head_size = inner_here // heads_here
    lag_rows = conv_inner.shape[0] - 1
    block_ids = jnp.arange(total_blocks, dtype=jnp.int32)
    same_owner = block_owner[:, None] == block_owner[None, :]
    first_block = jnp.min(jnp.where(same_owner, block_ids[None, :], total_blocks), axis=1)
    starting = (first_block == block_ids).astype(jnp.int32)
    request_ids = jnp.arange(lengths.shape[0], dtype=jnp.int32)
    own_length = jnp.sum(
        jnp.where(block_owner[:, None] == request_ids[None, :], lengths[None, :], 0), axis=1
    )
    valid_rows = jnp.clip(own_length - (block_ids - first_block) * BLOCK, 0, BLOCK)
    seq_index = lax.axis_index(SEQ)
    local_start = lax.dynamic_slice_in_dim(starting, seq_index * local_blocks, local_blocks)
    local_valid = lax.dynamic_slice_in_dim(valid_rows, seq_index * local_blocks, local_blocks)
    in_block = jnp.arange(row_count, dtype=jnp.int32) % BLOCK
    carry_on = jnp.repeat(local_start == 0, BLOCK)
    tp_count = lax.axis_size("tp")
    whole = gathered(tokens, "tp", 1)
    first_cols = jnp.concatenate([w_inner[:, 1, :], w_states, w_step], axis=1)
    first_weights = gathered(gathered(first_cols, "sz", 0), "sx", 0)
    late_cols = jnp.concatenate([w_inner[:, 0, :], w_output.T], axis=1)
    late_weights = lax.all_gather(late_cols, SEQ, axis=0, tiled=True)
    gate_weights = late_weights[:, :inner_here]
    out_weights = late_weights[:, inner_here:]
    first_sum = jnp.dot(whole, first_weights, preferred_element_type=jnp.float32)
    projected = first_sum.astype(jnp.bfloat16)
    x_in = projected[:, :inner_here]
    bc_in = projected[:, inner_here : inner_here + 2 * state_size]
    step_raw = projected[:, inner_here + 2 * state_size :]
    gate_in = jnp.dot(whole, gate_weights, preferred_element_type=jnp.float32).astype(jnp.bfloat16)
    edge_inner, edge_states = passed_along(
        (x_in[row_count - lag_rows :], bc_in[row_count - lag_rows :]), SEQ, 1
    )
    x_conv = convolve(x_in, edge_inner, conv_inner, in_block, carry_on)
    bc_conv = convolve(bc_in, edge_states, conv_states, in_block, carry_on)
    step_size = jax.nn.softplus(step_raw.astype(jnp.float32) + step_bias)
    log_decay = -decay_rate * step_size
    x_heads = x_conv.reshape(local_blocks, BLOCK, heads_here, head_size)
    b_rows = bc_conv[:, :state_size].reshape(local_blocks, BLOCK, state_size)
    c_rows = bc_conv[:, state_size:].reshape(local_blocks, BLOCK, state_size)
    step_blocks = step_size.reshape(local_blocks, BLOCK, heads_here)
    cumulative = jnp.cumsum(log_decay.reshape(local_blocks, BLOCK, heads_here), axis=1)
    causal = jnp.arange(BLOCK)[:, None] >= jnp.arange(BLOCK)[None, :]
    spread = cumulative[:, :, None, :] - cumulative[:, None, :, :]
    decays = jnp.exp(jnp.where(causal[None, :, :, None], spread, -jnp.inf))
    intersection = jnp.einsum("cin,cjn->cij", c_rows, b_rows, preferred_element_type=jnp.float32)
    mixing = (decays * intersection[:, :, :, None] * step_blocks[:, None, :, :]).astype(
        jnp.bfloat16
    )
    y_inner = jnp.einsum("cijh,cjhp->cihp", mixing, x_heads, preferred_element_type=jnp.float32)
    final_log = cumulative[:, -1, :]
    tail_weight = jnp.exp(final_log[:, None, :] - cumulative) * step_blocks
    weighted_b = (tail_weight[:, :, :, None] * b_rows.astype(jnp.float32)[:, :, None, :]).astype(
        jnp.bfloat16
    )
    fresh = jnp.einsum("cjhn,cjhp->chnp", weighted_b, x_heads, preferred_element_type=jnp.float32)
    keep_flag = jnp.where(local_start == 1, 0.0, 1.0).astype(jnp.float32)
    block_gain_each = jnp.exp(final_log) * keep_flag[:, None]

    block_gain = jnp.ones((heads_here,), jnp.float32)
    block_state = jnp.zeros((heads_here, state_size, head_size), jnp.float32)
    gains_in, states_in = [], []
    for block in range(local_blocks):
        gains_in.append(block_gain * keep_flag[block])
        states_in.append(block_state * keep_flag[block])
        block_gain = block_gain * block_gain_each[block]
        block_state = block_gain_each[block][:, None, None] * block_state + fresh[block]

    def packed(gain, state):
        rows = jnp.broadcast_to(gain[:, None, None], (heads_here, 1, head_size))
        return jnp.concatenate([state, rows], axis=1)

    prefix = passed_along(packed(block_gain, block_state), SEQ, 1)
    needed = min(-(-(LONGEST - 1) // local_blocks), lax.axis_size(SEQ) - 1)
    reach = 1
    while reach < needed:
        earlier = passed_along(prefix, SEQ, reach)
        gain_now = prefix[:, state_size:, :1]
        prefix = jnp.concatenate(
            [
                gain_now * earlier[:, :state_size] + prefix[:, :state_size],
                gain_now * earlier[:, state_size:],
            ],
            axis=1,
        )
        reach *= 2
    entering = prefix[:, :state_size]
    incoming_all = (
        jnp.stack(gains_in)[:, :, None, None] * entering[None] + jnp.stack(states_in)
    )
    incoming_half = incoming_all.astype(jnp.bfloat16)
    y_carry = jnp.exp(cumulative)[:, :, :, None] * jnp.einsum(
        "cin,chnp->cihp", c_rows, incoming_half, preferred_element_type=jnp.float32
    )
    y_total = (y_inner + y_carry).reshape(row_count, inner_here) + jnp.repeat(skip_gain, head_size)[
        None, :
    ] * x_conv.astype(jnp.float32)
    gated = y_total * jax.nn.silu(gate_in.astype(jnp.float32))
    squares = jnp.sum(gated * gated, axis=1)
    scaled = (gated * norm_gain).astype(jnp.bfloat16)
    partial_out = lax.dot_general(
        scaled, out_weights, (((1,), (1,)), ((), ())), preferred_element_type=jnp.float32
    )
    cols_here = partial_out.shape[1] // tp_count
    square_rows = jnp.tile(squares.reshape(row_count // cols_here, cols_here), (1, tp_count))
    summed = lax.psum_scatter(
        jnp.concatenate([partial_out, square_rows], axis=0), "tp", scatter_dimension=1, tiled=True
    )
    square_mean = summed[row_count:].reshape(row_count) / (inner_here * tp_count)
    mixed = summed[:row_count] * lax.rsqrt(square_mean + 1e-05)[:, None]
    live = in_block < jnp.repeat(local_valid, BLOCK)
    return jnp.where(live[:, None], mixed, 0.0).astype(jnp.bfloat16)


def solution(mesh):
    seq_count, tp_count = mesh.devices.shape
    split = Mesh(
        mesh.devices.reshape(seq_count // SEQ_INNER, SEQ_INNER, tp_count), ("sx", "sz", "tp")
    )
    return jax.shard_map(
        on_device,
        mesh=split,
        in_specs=(
            P(SEQ, "tp"),
            P(SEQ, None, "tp"),
            P(SEQ, None),
            P(SEQ, "tp"),
            P(None, "tp"),
            P(),
            P("tp"),
            P("tp"),
            P("tp"),
            P("tp"),
            P("tp", SEQ),
            P(),
            P(),
        ),
        out_specs=P(SEQ, "tp"),
        check_vma=False,
    )
```

```python
import jax
import jax.numpy as jnp
from jax import lax
from jax.sharding import PartitionSpec as P

BLOCK = 256
LONGEST = 64


def passed_along(value, axis, by):
    count = lax.axis_size(axis)
    pairs = [(i, i + by) for i in range(count) if 0 <= i + by < count]
    return lax.ppermute(value, axis, pairs)


def convolve(values, edge_rows, weights, in_block, carry_on):
    lag_rows = weights.shape[0] - 1
    row_total = values.shape[0]
    widened = jnp.concatenate([edge_rows, values], axis=0).astype(jnp.float32)
    total = jnp.zeros(values.shape, jnp.float32)
    for offset in range(weights.shape[0]):
        shifted = widened[lag_rows - offset : lag_rows - offset + row_total]
        keeping = (in_block >= offset) | carry_on
        total = total + jnp.where(keeping[:, None], shifted, 0.0) * weights[offset]
    return jax.nn.silu(total).astype(jnp.bfloat16)


def on_device(
    tokens,
    w_inner,
    w_states,
    w_step,
    conv_inner,
    conv_states,
    decay_rate,
    step_bias,
    skip_gain,
    norm_gain,
    w_output,
    block_owner,
    lengths,
):
    row_count = tokens.shape[0]
    local_blocks = row_count // BLOCK
    total_blocks = block_owner.shape[0]
    heads_here = w_step.shape[1]
    inner_here = w_inner.shape[2]
    state_size = w_states.shape[1] // 2
    head_size = inner_here // heads_here
    lag_rows = conv_inner.shape[0] - 1
    block_ids = jnp.arange(total_blocks, dtype=jnp.int32)
    same_owner = block_owner[:, None] == block_owner[None, :]
    first_block = jnp.min(jnp.where(same_owner, block_ids[None, :], total_blocks), axis=1)
    starting = (first_block == block_ids).astype(jnp.int32)
    request_ids = jnp.arange(lengths.shape[0], dtype=jnp.int32)
    own_length = jnp.sum(
        jnp.where(block_owner[:, None] == request_ids[None, :], lengths[None, :], 0), axis=1
    )
    valid_rows = jnp.clip(own_length - (block_ids - first_block) * BLOCK, 0, BLOCK)
    seq_index = lax.axis_index("seq")
    local_start = lax.dynamic_slice_in_dim(starting, seq_index * local_blocks, local_blocks)
    local_valid = lax.dynamic_slice_in_dim(valid_rows, seq_index * local_blocks, local_blocks)
    in_block = jnp.arange(row_count, dtype=jnp.int32) % BLOCK
    carry_on = jnp.repeat(local_start == 0, BLOCK)
    tp_count = lax.axis_size("tp")
    tp_index = lax.axis_index("tp")
    token_cols = tokens.shape[1]
    whole = jnp.zeros((row_count, token_cols * tp_count), tokens.dtype)
    whole = lax.dynamic_update_slice_in_dim(whole, tokens, tp_index * token_cols, axis=1)
    for shift in range(1, tp_count):
        arrived = lax.ppermute(
            tokens, "tp", [(i, (i + shift) % tp_count) for i in range(tp_count)]
        )
        origin = (tp_index + tp_count - shift) % tp_count
        whole = lax.dynamic_update_slice_in_dim(whole, arrived, origin * token_cols, axis=1)
    first_cols = jnp.concatenate([w_inner[:, 1, :], w_states, w_step], axis=1)
    first_weights = lax.all_gather(first_cols, "seq", axis=0, tiled=True)
    late_cols = jnp.concatenate([w_inner[:, 0, :], w_output.T], axis=1)
    late_weights = lax.all_gather(late_cols, "seq", axis=0, tiled=True)
    gate_weights = late_weights[:, :inner_here]
    out_weights = late_weights[:, inner_here:]
    first_sum = jnp.dot(whole, first_weights, preferred_element_type=jnp.float32)
    projected = first_sum.astype(jnp.bfloat16)
    x_in = projected[:, :inner_here]
    bc_in = projected[:, inner_here : inner_here + 2 * state_size]
    step_raw = projected[:, inner_here + 2 * state_size :]
    gate_in = jnp.dot(whole, gate_weights, preferred_element_type=jnp.float32).astype(jnp.bfloat16)
    edge_inner, edge_states = passed_along(
        (x_in[row_count - lag_rows :], bc_in[row_count - lag_rows :]), "seq", 1
    )
    x_conv = convolve(x_in, edge_inner, conv_inner, in_block, carry_on)
    bc_conv = convolve(bc_in, edge_states, conv_states, in_block, carry_on)
    step_size = jax.nn.softplus(step_raw.astype(jnp.float32) + step_bias)
    log_decay = -decay_rate * step_size
    x_heads = x_conv.reshape(local_blocks, BLOCK, heads_here, head_size)
    b_rows = bc_conv[:, :state_size].reshape(local_blocks, BLOCK, state_size)
    c_rows = bc_conv[:, state_size:].reshape(local_blocks, BLOCK, state_size)
    step_blocks = step_size.reshape(local_blocks, BLOCK, heads_here)
    cumulative = jnp.cumsum(log_decay.reshape(local_blocks, BLOCK, heads_here), axis=1)
    causal = jnp.arange(BLOCK)[:, None] >= jnp.arange(BLOCK)[None, :]
    spread = cumulative[:, :, None, :] - cumulative[:, None, :, :]
    decays = jnp.exp(jnp.where(causal[None, :, :, None], spread, -jnp.inf))
    intersection = jnp.einsum("cin,cjn->cij", c_rows, b_rows, preferred_element_type=jnp.float32)
    mixing = (decays * intersection[:, :, :, None] * step_blocks[:, None, :, :]).astype(
        jnp.bfloat16
    )
    y_inner = jnp.einsum("cijh,cjhp->cihp", mixing, x_heads, preferred_element_type=jnp.float32)
    final_log = cumulative[:, -1, :]
    tail_weight = jnp.exp(final_log[:, None, :] - cumulative) * step_blocks
    weighted_b = (tail_weight[:, :, :, None] * b_rows.astype(jnp.float32)[:, :, None, :]).astype(
        jnp.bfloat16
    )
    fresh = jnp.einsum("cjhn,cjhp->chnp", weighted_b, x_heads, preferred_element_type=jnp.float32)
    keep_flag = jnp.where(local_start == 1, 0.0, 1.0).astype(jnp.float32)
    block_gain_each = jnp.exp(final_log) * keep_flag[:, None]

    block_gain = jnp.ones((heads_here,), jnp.float32)
    block_state = jnp.zeros((heads_here, state_size, head_size), jnp.float32)
    gains_in, states_in = [], []
    for block in range(local_blocks):
        gains_in.append(block_gain * keep_flag[block])
        states_in.append(block_state * keep_flag[block])
        block_gain = block_gain * block_gain_each[block]
        block_state = block_gain_each[block][:, None, None] * block_state + fresh[block]

    def packed(gain, state):
        rows = jnp.broadcast_to(gain[:, None, None], (heads_here, 1, head_size))
        return jnp.concatenate([state, rows], axis=1)

    prefix = passed_along(packed(block_gain, block_state), "seq", 1)
    needed = min(-(-(LONGEST - 1) // local_blocks), lax.axis_size("seq") - 1)
    reach = 1
    while reach < needed:
        earlier = passed_along(prefix, "seq", reach)
        gain_now = prefix[:, state_size:, :1]
        prefix = jnp.concatenate(
            [
                gain_now * earlier[:, :state_size] + prefix[:, :state_size],
                gain_now * earlier[:, state_size:],
            ],
            axis=1,
        )
        reach *= 2
    entering = prefix[:, :state_size]
    incoming_all = (
        jnp.stack(gains_in)[:, :, None, None] * entering[None] + jnp.stack(states_in)
    )
    incoming_half = incoming_all.astype(jnp.bfloat16)
    y_carry = jnp.exp(cumulative)[:, :, :, None] * jnp.einsum(
        "cin,chnp->cihp", c_rows, incoming_half, preferred_element_type=jnp.float32
    )
    y_total = (y_inner + y_carry).reshape(row_count, inner_here) + jnp.repeat(skip_gain, head_size)[
        None, :
    ] * x_conv.astype(jnp.float32)
    gated = y_total * jax.nn.silu(gate_in.astype(jnp.float32))
    squares = jnp.sum(gated * gated, axis=1)
    scaled = (gated * norm_gain).astype(jnp.bfloat16)
    partial_out = lax.dot_general(
        scaled, out_weights, (((1,), (1,)), ((), ())), preferred_element_type=jnp.float32
    )
    cols_here = partial_out.shape[1] // tp_count
    square_rows = jnp.tile(squares.reshape(row_count // cols_here, cols_here), (1, tp_count))
    summed = lax.psum_scatter(
        jnp.concatenate([partial_out, square_rows], axis=0).astype(jnp.bfloat16),
        "tp",
        scatter_dimension=1,
        tiled=True,
    ).astype(jnp.float32)
    square_mean = summed[row_count:].reshape(row_count) / (inner_here * tp_count)
    mixed = summed[:row_count] * lax.rsqrt(square_mean + 1e-05)[:, None]
    live = in_block < jnp.repeat(local_valid, BLOCK)
    return jnp.where(live[:, None], mixed, 0.0).astype(jnp.bfloat16)


def solution(mesh):
    return jax.shard_map(
        on_device,
        mesh=mesh,
        in_specs=(
            P("seq", "tp"),
            P("seq", None, "tp"),
            P("seq", None),
            P("seq", "tp"),
            P(None, "tp"),
            P(),
            P("tp"),
            P("tp"),
            P("tp"),
            P("tp"),
            P("tp", "seq"),
            P(),
            P(),
        ),
        out_specs=P("seq", "tp"),
        check_vma=False,
    )
```

```python
import jax
import jax.numpy as jnp
from jax import lax
from jax.sharding import PartitionSpec as P

BLOCK = 256
LONGEST = 64


def passed_along(value, axis, by):
    count = lax.axis_size(axis)
    pairs = [(i, i + by) for i in range(count) if 0 <= i + by < count]
    return lax.ppermute(value, axis, pairs)


def convolve(values, edge_rows, weights, in_block, carry_on):
    lag_rows = weights.shape[0] - 1
    row_total = values.shape[0]
    widened = jnp.concatenate([edge_rows, values], axis=0).astype(jnp.float32)
    total = jnp.zeros(values.shape, jnp.float32)
    for offset in range(weights.shape[0]):
        shifted = widened[lag_rows - offset : lag_rows - offset + row_total]
        keeping = (in_block >= offset) | carry_on
        total = total + jnp.where(keeping[:, None], shifted, 0.0) * weights[offset]
    return jax.nn.silu(total).astype(jnp.bfloat16)


def on_device(
    tokens,
    w_inner,
    w_states,
    w_step,
    conv_inner,
    conv_states,
    decay_rate,
    step_bias,
    skip_gain,
    norm_gain,
    w_output,
    block_owner,
    lengths,
):
    row_count = tokens.shape[0]
    local_blocks = row_count // BLOCK
    total_blocks = block_owner.shape[0]
    heads_here = w_step.shape[1]
    inner_here = w_inner.shape[2]
    state_size = w_states.shape[1] // 2
    head_size = inner_here // heads_here
    lag_rows = conv_inner.shape[0] - 1
    block_ids = jnp.arange(total_blocks, dtype=jnp.int32)
    same_owner = block_owner[:, None] == block_owner[None, :]
    first_block = jnp.min(jnp.where(same_owner, block_ids[None, :], total_blocks), axis=1)
    starting = (first_block == block_ids).astype(jnp.int32)
    request_ids = jnp.arange(lengths.shape[0], dtype=jnp.int32)
    own_length = jnp.sum(
        jnp.where(block_owner[:, None] == request_ids[None, :], lengths[None, :], 0), axis=1
    )
    valid_rows = jnp.clip(own_length - (block_ids - first_block) * BLOCK, 0, BLOCK)
    seq_index = lax.axis_index("seq")
    local_start = lax.dynamic_slice_in_dim(starting, seq_index * local_blocks, local_blocks)
    local_valid = lax.dynamic_slice_in_dim(valid_rows, seq_index * local_blocks, local_blocks)
    in_block = jnp.arange(row_count, dtype=jnp.int32) % BLOCK
    carry_on = jnp.repeat(local_start == 0, BLOCK)
    tp_count = lax.axis_size("tp")
    tp_index = lax.axis_index("tp")
    token_cols = tokens.shape[1]
    whole = jnp.zeros((row_count, token_cols * tp_count), tokens.dtype)
    whole = lax.dynamic_update_slice_in_dim(whole, tokens, tp_index * token_cols, axis=1)
    for shift in range(1, tp_count):
        arrived = lax.ppermute(
            tokens, "tp", [(i, (i + shift) % tp_count) for i in range(tp_count)]
        )
        origin = (tp_index + tp_count - shift) % tp_count
        whole = lax.dynamic_update_slice_in_dim(whole, arrived, origin * token_cols, axis=1)
    first_cols = jnp.concatenate([w_inner[:, 1, :], w_states, w_step], axis=1)
    first_weights = lax.all_gather(first_cols, "seq", axis=0, tiled=True)
    late_cols = jnp.concatenate([w_inner[:, 0, :], w_output.T], axis=1)
    late_weights = lax.all_gather(late_cols, "seq", axis=0, tiled=True)
    gate_weights = late_weights[:, :inner_here]
    out_weights = late_weights[:, inner_here:]
    first_sum = jnp.dot(whole, first_weights, preferred_element_type=jnp.float32)
    projected = first_sum.astype(jnp.bfloat16)
    x_in = projected[:, :inner_here]
    bc_in = projected[:, inner_here : inner_here + 2 * state_size]
    step_raw = projected[:, inner_here + 2 * state_size :]
    gate_in = jnp.dot(whole, gate_weights, preferred_element_type=jnp.float32).astype(jnp.bfloat16)
    edge_inner, edge_states = passed_along(
        (x_in[row_count - lag_rows :], bc_in[row_count - lag_rows :]), "seq", 1
    )
    x_conv = convolve(x_in, edge_inner, conv_inner, in_block, carry_on)
    bc_conv = convolve(bc_in, edge_states, conv_states, in_block, carry_on)
    step_size = jax.nn.softplus(step_raw.astype(jnp.float32) + step_bias)
    log_decay = -decay_rate * step_size
    x_heads = x_conv.reshape(local_blocks, BLOCK, heads_here, head_size)
    b_rows = bc_conv[:, :state_size].reshape(local_blocks, BLOCK, state_size)
    c_rows = bc_conv[:, state_size:].reshape(local_blocks, BLOCK, state_size)
    step_blocks = step_size.reshape(local_blocks, BLOCK, heads_here)
    cumulative = jnp.cumsum(log_decay.reshape(local_blocks, BLOCK, heads_here), axis=1)
    causal = jnp.arange(BLOCK)[:, None] >= jnp.arange(BLOCK)[None, :]
    spread = cumulative[:, :, None, :] - cumulative[:, None, :, :]
    decays = jnp.exp(jnp.where(causal[None, :, :, None], spread, -jnp.inf))
    intersection = jnp.einsum("cin,cjn->cij", c_rows, b_rows, preferred_element_type=jnp.float32)
    mixing = (decays * intersection[:, :, :, None] * step_blocks[:, None, :, :]).astype(
        jnp.bfloat16
    )
    y_inner = jnp.einsum("cijh,cjhp->cihp", mixing, x_heads, preferred_element_type=jnp.float32)
    final_log = cumulative[:, -1, :]
    tail_weight = jnp.exp(final_log[:, None, :] - cumulative) * step_blocks
    weighted_b = (tail_weight[:, :, :, None] * b_rows.astype(jnp.float32)[:, :, None, :]).astype(
        jnp.bfloat16
    )
    fresh = jnp.einsum("cjhn,cjhp->chnp", weighted_b, x_heads, preferred_element_type=jnp.float32)
    keep_flag = jnp.where(local_start == 1, 0.0, 1.0).astype(jnp.float32)
    block_gain_each = jnp.exp(final_log) * keep_flag[:, None]

    block_gain = jnp.ones((heads_here,), jnp.float32)
    block_state = jnp.zeros((heads_here, state_size, head_size), jnp.float32)
    gains_in, states_in = [], []
    for block in range(local_blocks):
        gains_in.append(block_gain * keep_flag[block])
        states_in.append(block_state * keep_flag[block])
        block_gain = block_gain * block_gain_each[block]
        block_state = block_gain_each[block][:, None, None] * block_state + fresh[block]

    def packed(gain, state):
        rows = jnp.broadcast_to(gain[:, None, None], (heads_here, 1, head_size))
        return jnp.concatenate([state, rows], axis=1)

    prefix = passed_along(packed(block_gain, block_state), "seq", 1)
    needed = min(-(-(LONGEST - 1) // local_blocks), lax.axis_size("seq") - 1)
    reach = 1
    while reach < needed:
        earlier = passed_along(prefix, "seq", reach)
        gain_now = prefix[:, state_size:, :1]
        prefix = jnp.concatenate(
            [
                gain_now * earlier[:, :state_size] + prefix[:, :state_size],
                gain_now * earlier[:, state_size:],
            ],
            axis=1,
        )
        reach *= 2
    entering = prefix[:, :state_size]
    incoming_all = (
        jnp.stack(gains_in)[:, :, None, None] * entering[None] + jnp.stack(states_in)
    )
    incoming_half = incoming_all.astype(jnp.bfloat16)
    y_carry = jnp.exp(cumulative)[:, :, :, None] * jnp.einsum(
        "cin,chnp->cihp", c_rows, incoming_half, preferred_element_type=jnp.float32
    )
    y_total = (y_inner + y_carry).reshape(row_count, inner_here) + jnp.repeat(skip_gain, head_size)[
        None, :
    ] * x_conv.astype(jnp.float32)
    gated = y_total * jax.nn.silu(gate_in.astype(jnp.float32))
    tp_count = lax.axis_size("tp")
    squares = lax.psum(jnp.sum(gated * gated, axis=1), "tp")
    square_mean = squares / (inner_here * tp_count)
    normed = (gated * lax.rsqrt(square_mean + 1e-05)[:, None] * norm_gain).astype(jnp.bfloat16)
    partial_out = lax.dot_general(
        normed, out_weights, (((1,), (1,)), ((), ())), preferred_element_type=jnp.float32
    )
    mixed = lax.psum_scatter(
        partial_out.astype(jnp.bfloat16), "tp", scatter_dimension=1, tiled=True
    )
    live = in_block < jnp.repeat(local_valid, BLOCK)
    return jnp.where(live[:, None], mixed, 0.0).astype(jnp.bfloat16)


def solution(mesh):
    return jax.shard_map(
        on_device,
        mesh=mesh,
        in_specs=(
            P("seq", "tp"),
            P("seq", None, "tp"),
            P("seq", None),
            P("seq", "tp"),
            P(None, "tp"),
            P(),
            P("tp"),
            P("tp"),
            P("tp"),
            P("tp"),
            P("tp", "seq"),
            P(),
            P(),
        ),
        out_specs=P("seq", "tp"),
        check_vma=False,
    )
```

```python
import jax
import jax.numpy as jnp
from jax import lax
from jax.sharding import PartitionSpec as P

BLOCK = 256
LONGEST = 64


def passed_along(value, axis, by):
    count = lax.axis_size(axis)
    pairs = [(i, i + by) for i in range(count) if 0 <= i + by < count]
    return lax.ppermute(value, axis, pairs)


def convolve(values, edge_rows, weights, in_block, carry_on):
    lag_rows = weights.shape[0] - 1
    row_total = values.shape[0]
    widened = jnp.concatenate([edge_rows, values], axis=0).astype(jnp.float32)
    total = jnp.zeros(values.shape, jnp.float32)
    for offset in range(weights.shape[0]):
        shifted = widened[lag_rows - offset : lag_rows - offset + row_total]
        keeping = (in_block >= offset) | carry_on
        total = total + jnp.where(keeping[:, None], shifted, 0.0) * weights[offset]
    return jax.nn.silu(total).astype(jnp.bfloat16)


def on_device(
    tokens,
    w_inner,
    w_states,
    w_step,
    conv_inner,
    conv_states,
    decay_rate,
    step_bias,
    skip_gain,
    norm_gain,
    w_output,
    block_owner,
    lengths,
):
    row_count = tokens.shape[0]
    local_blocks = row_count // BLOCK
    total_blocks = block_owner.shape[0]
    heads_here = w_step.shape[1]
    inner_here = w_inner.shape[2]
    state_size = w_states.shape[1] // 2
    head_size = inner_here // heads_here
    lag_rows = conv_inner.shape[0] - 1
    block_ids = jnp.arange(total_blocks, dtype=jnp.int32)
    same_owner = block_owner[:, None] == block_owner[None, :]
    first_block = jnp.min(jnp.where(same_owner, block_ids[None, :], total_blocks), axis=1)
    starting = (first_block == block_ids).astype(jnp.int32)
    request_ids = jnp.arange(lengths.shape[0], dtype=jnp.int32)
    own_length = jnp.sum(
        jnp.where(block_owner[:, None] == request_ids[None, :], lengths[None, :], 0), axis=1
    )
    valid_rows = jnp.clip(own_length - (block_ids - first_block) * BLOCK, 0, BLOCK)
    seq_index = lax.axis_index("seq")
    local_start = lax.dynamic_slice_in_dim(starting, seq_index * local_blocks, local_blocks)
    local_valid = lax.dynamic_slice_in_dim(valid_rows, seq_index * local_blocks, local_blocks)
    in_block = jnp.arange(row_count, dtype=jnp.int32) % BLOCK
    carry_on = jnp.repeat(local_start == 0, BLOCK)
    tp_count = lax.axis_size("tp")
    tp_index = lax.axis_index("tp")
    token_cols = tokens.shape[1]
    whole = jnp.zeros((row_count, token_cols * tp_count), tokens.dtype)
    whole = lax.dynamic_update_slice_in_dim(whole, tokens, tp_index * token_cols, axis=1)
    for shift in range(1, tp_count):
        arrived = lax.ppermute(
            tokens, "tp", [(i, (i + shift) % tp_count) for i in range(tp_count)]
        )
        origin = (tp_index + tp_count - shift) % tp_count
        whole = lax.dynamic_update_slice_in_dim(whole, arrived, origin * token_cols, axis=1)
    first_cols = jnp.concatenate([w_inner[:, 1, :], w_states, w_step], axis=1)
    first_weights = lax.all_gather(first_cols, "seq", axis=0, tiled=True)
    late_cols = jnp.concatenate([w_inner[:, 0, :], w_output.T], axis=1)
    late_weights = lax.all_gather(late_cols, "seq", axis=0, tiled=True)
    gate_weights = late_weights[:, :inner_here]
    out_weights = late_weights[:, inner_here:]
    first_sum = jnp.dot(whole, first_weights, preferred_element_type=jnp.float32)
    projected = first_sum.astype(jnp.bfloat16)
    x_in = projected[:, :inner_here]
    bc_in = projected[:, inner_here : inner_here + 2 * state_size]
    step_raw = projected[:, inner_here + 2 * state_size :]
    gate_in = jnp.dot(whole, gate_weights, preferred_element_type=jnp.float32).astype(jnp.bfloat16)
    edge_inner, edge_states = passed_along(
        (x_in[row_count - lag_rows :], bc_in[row_count - lag_rows :]), "seq", 1
    )
    x_conv = convolve(x_in, edge_inner, conv_inner, in_block, carry_on)
    bc_conv = convolve(bc_in, edge_states, conv_states, in_block, carry_on)
    step_size = jax.nn.softplus(step_raw.astype(jnp.float32) + step_bias)
    log_decay = -decay_rate * step_size
    x_heads = x_conv.reshape(local_blocks, BLOCK, heads_here, head_size)
    b_rows = bc_conv[:, :state_size].reshape(local_blocks, BLOCK, state_size)
    c_rows = bc_conv[:, state_size:].reshape(local_blocks, BLOCK, state_size)
    step_blocks = step_size.reshape(local_blocks, BLOCK, heads_here)
    cumulative = jnp.cumsum(log_decay.reshape(local_blocks, BLOCK, heads_here), axis=1)
    causal = jnp.arange(BLOCK)[:, None] >= jnp.arange(BLOCK)[None, :]
    spread = cumulative[:, :, None, :] - cumulative[:, None, :, :]
    decays = jnp.exp(jnp.where(causal[None, :, :, None], spread, -jnp.inf))
    intersection = jnp.einsum("cin,cjn->cij", c_rows, b_rows, preferred_element_type=jnp.float32)
    mixing = (decays * intersection[:, :, :, None] * step_blocks[:, None, :, :]).astype(
        jnp.bfloat16
    )
    y_inner = jnp.einsum("cijh,cjhp->cihp", mixing, x_heads, preferred_element_type=jnp.float32)
    final_log = cumulative[:, -1, :]
    tail_weight = jnp.exp(final_log[:, None, :] - cumulative) * step_blocks
    weighted_b = (tail_weight[:, :, :, None] * b_rows.astype(jnp.float32)[:, :, None, :]).astype(
        jnp.bfloat16
    )
    fresh = jnp.einsum("cjhn,cjhp->chnp", weighted_b, x_heads, preferred_element_type=jnp.float32)
    keep_flag = jnp.where(local_start == 1, 0.0, 1.0).astype(jnp.float32)
    block_gain_each = jnp.exp(final_log) * keep_flag[:, None]

    block_gain = jnp.ones((heads_here,), jnp.float32)
    block_state = jnp.zeros((heads_here, state_size, head_size), jnp.float32)
    gains_in, states_in = [], []
    for block in range(local_blocks):
        gains_in.append(block_gain * keep_flag[block])
        states_in.append(block_state * keep_flag[block])
        block_gain = block_gain * block_gain_each[block]
        block_state = block_gain_each[block][:, None, None] * block_state + fresh[block]

    def packed(gain, state):
        rows = jnp.broadcast_to(gain[:, None, None], (heads_here, 1, head_size))
        return jnp.concatenate([state, rows], axis=1)

    def sent(value, by):
        return passed_along(value.astype(jnp.bfloat16), "seq", by).astype(jnp.float32)

    prefix = sent(packed(block_gain, block_state), 1)
    needed = min(-(-(LONGEST - 1) // local_blocks), lax.axis_size("seq") - 1)
    reach = 1
    while reach < needed:
        earlier = sent(prefix, reach)
        gain_now = prefix[:, state_size:, :1]
        prefix = jnp.concatenate(
            [
                gain_now * earlier[:, :state_size] + prefix[:, :state_size],
                gain_now * earlier[:, state_size:],
            ],
            axis=1,
        )
        reach *= 2
    entering = prefix[:, :state_size]
    incoming_all = (
        jnp.stack(gains_in)[:, :, None, None] * entering[None] + jnp.stack(states_in)
    )
    incoming_half = incoming_all.astype(jnp.bfloat16)
    y_carry = jnp.exp(cumulative)[:, :, :, None] * jnp.einsum(
        "cin,chnp->cihp", c_rows, incoming_half, preferred_element_type=jnp.float32
    )
    y_total = (y_inner + y_carry).reshape(row_count, inner_here) + jnp.repeat(skip_gain, head_size)[
        None, :
    ] * x_conv.astype(jnp.float32)
    gated = y_total * jax.nn.silu(gate_in.astype(jnp.float32))
    squares = jnp.sum(gated * gated, axis=1)
    scaled = (gated * norm_gain).astype(jnp.bfloat16)
    partial_out = lax.dot_general(
        scaled, out_weights, (((1,), (1,)), ((), ())), preferred_element_type=jnp.float32
    )
    cols_here = partial_out.shape[1] // tp_count
    square_rows = jnp.tile(squares.reshape(row_count // cols_here, cols_here), (1, tp_count))
    summed = lax.psum_scatter(
        jnp.concatenate([partial_out, square_rows], axis=0), "tp", scatter_dimension=1, tiled=True
    )
    square_mean = summed[row_count:].reshape(row_count) / (inner_here * tp_count)
    mixed = summed[:row_count] * lax.rsqrt(square_mean + 1e-05)[:, None]
    live = in_block < jnp.repeat(local_valid, BLOCK)
    return jnp.where(live[:, None], mixed, 0.0).astype(jnp.bfloat16)


def solution(mesh):
    return jax.shard_map(
        on_device,
        mesh=mesh,
        in_specs=(
            P("seq", "tp"),
            P("seq", None, "tp"),
            P("seq", None),
            P("seq", "tp"),
            P(None, "tp"),
            P(),
            P("tp"),
            P("tp"),
            P("tp"),
            P("tp"),
            P("tp", "seq"),
            P(),
            P(),
        ),
        out_specs=P("seq", "tp"),
        check_vma=False,
    )
```

```python
import jax
import jax.numpy as jnp
from jax import lax
from jax.sharding import PartitionSpec as P

BLOCK = 256
LONGEST = 64


def passed_along(value, axis, by):
    count = lax.axis_size(axis)
    pairs = [(i, i + by) for i in range(count) if 0 <= i + by < count]
    return lax.ppermute(value, axis, pairs)


def convolve(values, edge_rows, weights, in_block, carry_on):
    lag_rows = weights.shape[0] - 1
    row_total = values.shape[0]
    widened = jnp.concatenate([edge_rows, values], axis=0).astype(jnp.float32)
    total = jnp.zeros(values.shape, jnp.float32)
    for offset in range(weights.shape[0]):
        shifted = widened[lag_rows - offset : lag_rows - offset + row_total]
        keeping = (in_block >= offset) | carry_on
        total = total + jnp.where(keeping[:, None], shifted, 0.0) * weights[offset]
    return jax.nn.silu(total).astype(jnp.bfloat16)


def on_device(
    tokens,
    w_inner,
    w_states,
    w_step,
    conv_inner,
    conv_states,
    decay_rate,
    step_bias,
    skip_gain,
    norm_gain,
    w_output,
    block_owner,
    lengths,
):
    row_count = tokens.shape[0]
    local_blocks = row_count // BLOCK
    total_blocks = block_owner.shape[0]
    heads_here = w_step.shape[1]
    inner_here = w_inner.shape[2]
    state_size = w_states.shape[1] // 2
    head_size = inner_here // heads_here
    lag_rows = conv_inner.shape[0] - 1
    block_ids = jnp.arange(total_blocks, dtype=jnp.int32)
    same_owner = block_owner[:, None] == block_owner[None, :]
    first_block = jnp.min(jnp.where(same_owner, block_ids[None, :], total_blocks), axis=1)
    starting = (first_block == block_ids).astype(jnp.int32)
    request_ids = jnp.arange(lengths.shape[0], dtype=jnp.int32)
    own_length = jnp.sum(
        jnp.where(block_owner[:, None] == request_ids[None, :], lengths[None, :], 0), axis=1
    )
    valid_rows = jnp.clip(own_length - (block_ids - first_block) * BLOCK, 0, BLOCK)
    seq_index = lax.axis_index("seq")
    local_start = lax.dynamic_slice_in_dim(starting, seq_index * local_blocks, local_blocks)
    local_valid = lax.dynamic_slice_in_dim(valid_rows, seq_index * local_blocks, local_blocks)
    in_block = jnp.arange(row_count, dtype=jnp.int32) % BLOCK
    carry_on = jnp.repeat(local_start == 0, BLOCK)
    tp_count = lax.axis_size("tp")
    tp_index = lax.axis_index("tp")
    token_cols = tokens.shape[1]
    whole = jnp.zeros((row_count, token_cols * tp_count), tokens.dtype)
    whole = lax.dynamic_update_slice_in_dim(whole, tokens, tp_index * token_cols, axis=1)
    for shift in range(1, tp_count):
        arrived = lax.ppermute(
            tokens, "tp", [(i, (i + shift) % tp_count) for i in range(tp_count)]
        )
        origin = (tp_index + tp_count - shift) % tp_count
        whole = lax.dynamic_update_slice_in_dim(whole, arrived, origin * token_cols, axis=1)
    first_cols = jnp.concatenate([w_inner[:, 1, :], w_states, w_step], axis=1)
    first_weights = lax.all_gather(first_cols, "seq", axis=0, tiled=True)
    late_cols = jnp.concatenate([w_inner[:, 0, :], w_output.T], axis=1)
    late_weights = lax.all_gather(late_cols, "seq", axis=0, tiled=True)
    gate_weights = late_weights[:, :inner_here]
    out_weights = late_weights[:, inner_here:]
    first_sum = jnp.dot(whole, first_weights, preferred_element_type=jnp.float32)
    projected = first_sum.astype(jnp.bfloat16)
    x_in = projected[:, :inner_here]
    bc_in = projected[:, inner_here : inner_here + 2 * state_size]
    step_raw = projected[:, inner_here + 2 * state_size :]
    gate_in = jnp.dot(whole, gate_weights, preferred_element_type=jnp.float32).astype(jnp.bfloat16)
    edge_inner, edge_states = passed_along(
        (x_in[row_count - lag_rows :], bc_in[row_count - lag_rows :]), "seq", 1
    )
    x_conv = convolve(x_in, edge_inner, conv_inner, in_block, carry_on)
    bc_conv = convolve(bc_in, edge_states, conv_states, in_block, carry_on)
    step_size = jax.nn.softplus(step_raw.astype(jnp.float32) + step_bias)
    log_decay = -decay_rate * step_size
    x_heads = x_conv.reshape(local_blocks, BLOCK, heads_here, head_size)
    b_rows = bc_conv[:, :state_size].reshape(local_blocks, BLOCK, state_size)
    c_rows = bc_conv[:, state_size:].reshape(local_blocks, BLOCK, state_size)
    step_blocks = step_size.reshape(local_blocks, BLOCK, heads_here)
    cumulative = jnp.cumsum(log_decay.reshape(local_blocks, BLOCK, heads_here), axis=1)
    causal = jnp.arange(BLOCK)[:, None] >= jnp.arange(BLOCK)[None, :]
    spread = cumulative[:, :, None, :] - cumulative[:, None, :, :]
    decays = jnp.exp(jnp.where(causal[None, :, :, None], spread, -jnp.inf))
    intersection = jnp.einsum("cin,cjn->cij", c_rows, b_rows, preferred_element_type=jnp.float32)
    mixing = (decays * intersection[:, :, :, None] * step_blocks[:, None, :, :]).astype(
        jnp.bfloat16
    )
    y_inner = jnp.einsum("cijh,cjhp->cihp", mixing, x_heads, preferred_element_type=jnp.float32)
    final_log = cumulative[:, -1, :]
    tail_weight = jnp.exp(final_log[:, None, :] - cumulative) * step_blocks
    weighted_b = (tail_weight[:, :, :, None] * b_rows.astype(jnp.float32)[:, :, None, :]).astype(
        jnp.bfloat16
    )
    fresh = jnp.einsum("cjhn,cjhp->chnp", weighted_b, x_heads, preferred_element_type=jnp.float32)
    keep_flag = jnp.where(local_start == 1, 0.0, 1.0).astype(jnp.float32)
    block_gain_each = jnp.exp(final_log) * keep_flag[:, None]

    block_gain = jnp.ones((heads_here,), jnp.float32)
    block_state = jnp.zeros((heads_here, state_size, head_size), jnp.float32)
    gains_in, states_in = [], []
    for block in range(local_blocks):
        gains_in.append(block_gain * keep_flag[block])
        states_in.append(block_state * keep_flag[block])
        block_gain = block_gain * block_gain_each[block]
        block_state = block_gain_each[block][:, None, None] * block_state + fresh[block]

    def packed(gain, state):
        rows = jnp.broadcast_to(gain[:, None, None], (heads_here, 1, head_size))
        return jnp.concatenate([state, rows], axis=1)

    def sent(value, by):
        return passed_along(value.astype(jnp.bfloat16), "seq", by).astype(jnp.float32)

    prefix = sent(packed(block_gain, block_state), 1)
    needed = min(-(-(LONGEST - 1) // local_blocks), lax.axis_size("seq") - 1)
    reach = 1
    while reach < needed:
        earlier = sent(prefix, reach)
        gain_now = prefix[:, state_size:, :1]
        prefix = jnp.concatenate(
            [
                gain_now * earlier[:, :state_size] + prefix[:, :state_size],
                gain_now * earlier[:, state_size:],
            ],
            axis=1,
        )
        reach *= 2
    entering = prefix[:, :state_size]
    incoming_all = (
        jnp.stack(gains_in)[:, :, None, None] * entering[None] + jnp.stack(states_in)
    )
    incoming_half = incoming_all.astype(jnp.bfloat16)
    y_carry = jnp.exp(cumulative)[:, :, :, None] * jnp.einsum(
        "cin,chnp->cihp", c_rows, incoming_half, preferred_element_type=jnp.float32
    )
    y_total = (y_inner + y_carry).reshape(row_count, inner_here) + jnp.repeat(skip_gain, head_size)[
        None, :
    ] * x_conv.astype(jnp.float32)
    gated = y_total * jax.nn.silu(gate_in.astype(jnp.float32))
    squares = jnp.sum(gated * gated, axis=1)
    scaled = (gated * norm_gain).astype(jnp.bfloat16)
    cols_here = out_weights.shape[0] // tp_count
    square_rows = jnp.tile(squares.reshape(row_count // cols_here, cols_here), (1, tp_count))
    padded = jnp.concatenate(
        [scaled, jnp.zeros((square_rows.shape[0], inner_here), scaled.dtype)], axis=0
    )
    partial_out = lax.dot_general(
        padded, out_weights, (((1,), (1,)), ((), ())), preferred_element_type=jnp.float32
    )
    summed = lax.psum_scatter(
        lax.dynamic_update_slice_in_dim(partial_out, square_rows, row_count, axis=0),
        "tp",
        scatter_dimension=1,
        tiled=True,
    )
    square_mean = summed[row_count:].reshape(row_count) / (inner_here * tp_count)
    mixed = summed[:row_count] * lax.rsqrt(square_mean + 1e-05)[:, None]
    live = in_block < jnp.repeat(local_valid, BLOCK)
    return jnp.where(live[:, None], mixed, 0.0).astype(jnp.bfloat16)


def solution(mesh):
    return jax.shard_map(
        on_device,
        mesh=mesh,
        in_specs=(
            P("seq", "tp"),
            P("seq", None, "tp"),
            P("seq", None),
            P("seq", "tp"),
            P(None, "tp"),
            P(),
            P("tp"),
            P("tp"),
            P("tp"),
            P("tp"),
            P("tp", "seq"),
            P(),
            P(),
        ),
        out_specs=P("seq", "tp"),
        check_vma=False,
    )
```
